32 devices in a mesh: clips: 2 (over y), patch: 4 (over z), span: 2 (over x), chan: 2 (over core).
Axes of the slice: x: 2, y: 2, z: 4, core: 2. Of those that a mesh axis runs over, the one named last changes fastest.
Arguments:
- latent_tiles: bfloat16 [4, 256, 4, 384], P(('clips', 'span'), 'patch'), parts along dimension 0, may hold values from -12 to 12
- route: int32 [4, 256], P(('clips', 'span')), parts along dimension 0, may hold values from 0 to 255, as said below
- w_query: bfloat16 [384, 384], replicated, may hold values from -0.5 to 4.6
- w_keyval: bfloat16 [384, 768], replicated, may hold values from -0.5 to 4.6
- conv_weight: bfloat16 [3, 3, 3, 384, 384], P(None, None, None, None, 'chan'), may hold values from -0.0625 to 0.0625
Outputs:
- decoded: bfloat16 [8, 8, 64, 384], P(('clips', 'span'), 'patch', None, 'chan'), parts along dimension 0
The draws below stay inside these ranges and needn't reach their ends.
There are 2 independent parts, one for each index of `clips`. The reference program is written for one: setup_inputs(seed, part) draws one part's arguments, and reference() takes and returns one part's arrays. A program takes and returns all parts, laid end to end along the dimension named above; an argument that names none is the same for every part. Nothing has to cross between parts.
Inputs may be any that keep to these rules, and one draw needn't show every extreme that they name: `route`: each span's row is a permutation of 0 .. 255. The 64 tiles of positions j * 64 to (j + 1) * 64 - 1 go to at most 32 per owner, and in every span some such group sends exactly 32 to one owner.
All inputs are finite; a program needn't handle non-finite values.
Results may differ from the reference program's by a relative error of at most 0.0065.
Values may be sent and summed in bfloat16 or wider, within the bound.
No kernel may reach another device: no remote copies, remote signals or barrier semaphores. Data moves between devices by JAX's collectives and lax.ppermute only.
A program may use at most 64 MiB of HBM per device.

```python
import math
import jax
import jax.numpy as jnp
from jax import lax

C = 384
W = 64
RD = 2
FD = 2
TCELL = 4
SPANS = 2
FRAMES = 4
ROWS = 8
TPD = 64
TILES = 256


def route_block(key):
    patch_count = TILES // TPD
    per_device = TPD
    slot_count = 2 * per_device // patch_count
    keys_split = jax.random.split(key, 5)
    shift_order = jax.random.permutation(keys_split[0], patch_count).astype(jnp.int32)
    second = jax.random.randint(keys_split[1], (patch_count // 2,), 0, slot_count + 1)
    second = second.at[0].set(0)
    counts = jnp.zeros((patch_count,), jnp.int32)
    counts = counts.at[shift_order[0::2]].set(slot_count - second)
    counts = counts.at[shift_order[1::2]].set(second)
    bounds = jnp.cumsum(counts)
    positions = jnp.arange(per_device, dtype=jnp.int32)
    shift_list = jnp.sum((bounds[None, :] <= positions[:, None]).astype(jnp.int32), axis=1)
    owner_order = jax.random.permutation(keys_split[2], patch_count).astype(jnp.int32)
    sources = jnp.arange(patch_count, dtype=jnp.int32)
    destination = owner_order[(sources[:, None] + shift_list[None, :]) % patch_count]
    scores = jax.random.randint(keys_split[3], (patch_count, per_device), 0, 1 << 20) * per_device + positions[None, :]
    shuffle = jnp.argsort(scores, axis=1)
    owners = jnp.take_along_axis(destination, shuffle, axis=1).reshape(-1)
    priority = jax.random.permutation(keys_split[4], patch_count * per_device).astype(jnp.int32)
    same_owner = owners[:, None] == owners[None, :]
    before = priority[None, :] < priority[:, None]
    spot_ids = jnp.sum((same_owner & before).astype(jnp.int32), axis=1)
    return (owners * per_device + spot_ids).astype(jnp.int32)


def draw_route(key, part):
    return jax.vmap(route_block)(jax.random.split(key, SPANS))


def draw_latent_tiles(key, part):
    shape = (SPANS, TILES, TCELL, C)
    keys_split = jax.random.split(key, 1)
    values = jnp.clip(jax.random.normal(keys_split[0], shape, jnp.float32), -6.0, 6.0)
    return values.astype(jnp.bfloat16)


def draw_w_query(key, part):
    keys_split = jax.random.split(jax.random.fold_in(key, 11), 2)
    values = 0.08 * jnp.clip(jax.random.normal(keys_split[1], (C, C), jnp.float32), -6.0, 6.0)
    return values.astype(jnp.bfloat16)


def draw_w_keyval(key, part):
    keys_split = jax.random.split(jax.random.fold_in(key, 23), 3)
    values = 0.08 * jnp.clip(jax.random.normal(keys_split[2], (C, 2 * C), jnp.float32), -6.0, 6.0)
    return values.astype(jnp.bfloat16)


def shard_levels(own_key, dims, shards, low, top_value):
    def one(axis_at, blocks):
        draws = jax.random.uniform(jax.random.fold_in(jax.random.fold_in(own_key, 6), axis_at), (blocks,), jnp.float32, low / len(shards), top_value / len(shards))
        return jnp.repeat(jnp.exp(draws), dims[axis_at] // blocks).reshape((-1,) + (1,) * (len(dims) - axis_at - 1))

    level = one(*shards[0])
    for cut in shards[1:]:
        level = level * one(*cut)
    return level


def centred(key, dims, deviation, limit, pieces=(), kind=jnp.bfloat16):
    loudness = shard_levels(key, dims, pieces, -0.22, 0.18) if pieces else 1.0
    drawn = jax.random.normal(key, dims, jnp.float32) * deviation * loudness
    return jnp.minimum(jnp.maximum(drawn, -limit), limit).astype(kind)


def setup_inputs(seed: int = 0, part: int = 0) -> dict:
    key_list = jax.random.split(jax.random.key(seed), 6)
    part_splits = jax.random.split(jax.random.fold_in(key_list[5], part), 6)
    latent_tiles = draw_latent_tiles(jax.random.fold_in(jax.random.fold_in(key_list[5], part), 71), part)
    route = draw_route(jax.random.fold_in(jax.random.fold_in(key_list[5], part), 71), part)
    w_query = draw_w_query(jax.random.fold_in(key_list[5], 71), part)
    w_keyval = draw_w_keyval(jax.random.fold_in(key_list[5], 71), part)
    conv_weight = centred(key_list[4], (3, 3, 3, C, C), (27 * C) ** -0.5, 0.0625, ((4, 2),))
    return {"latent_tiles": latent_tiles, "route": route, "w_query": w_query, "w_keyval": w_keyval, "conv_weight": conv_weight}


epsilon = 1e-06

def scaled_rms(values):
    wide = values.astype(jnp.float32)
    return wide / jnp.sqrt(lax.optimization_barrier(jnp.mean(wide * wide, axis=-1, keepdims=True)) + epsilon)

def place_block(tile_block, table):
    inverse = jnp.argsort(table).astype(jnp.int32)
    return jnp.take(tile_block, inverse, axis=0)

def attend_frame(frame_pair):
    query_rows, keyval_rows = frame_pair
    width_c = query_rows.shape[-1]
    scores = jnp.dot(query_rows, keyval_rows[:, :width_c].T, preferred_element_type=jnp.float32) * (1.0 / math.sqrt(width_c))
    largest = lax.optimization_barrier(jnp.max(scores, axis=-1, keepdims=True))
    powers = jnp.exp(scores - largest)
    totals = lax.optimization_barrier(jnp.sum(powers, axis=-1, keepdims=True))
    weights = powers.astype(jnp.bfloat16)
    return jnp.dot(weights, keyval_rows[:, width_c:], preferred_element_type=jnp.float32) / totals

def reference(latent_tiles, route, w_query, w_keyval, conv_weight):
    placed = jax.vmap(place_block)(latent_tiles, route)
    placed = placed.reshape(SPANS, ROWS // RD, FD, RD, W // TCELL, TCELL, C)
    features = placed.transpose(0, 2, 1, 3, 4, 5, 6).reshape(FRAMES, ROWS, W, C)
    normed = scaled_rms(features).astype(jnp.bfloat16)
    flat_cells = normed.reshape(FRAMES * ROWS * W, C)
    queries = jnp.dot(flat_cells, w_query, preferred_element_type=jnp.float32).astype(jnp.bfloat16)
    keyvals = jnp.dot(flat_cells, w_keyval, preferred_element_type=jnp.float32).astype(jnp.bfloat16)
    attended = lax.map(attend_frame, (queries.reshape(FRAMES, ROWS * W, C), keyvals.reshape(FRAMES, ROWS * W, 2 * C)))
    mixed = (features.astype(jnp.float32) + attended.reshape(FRAMES, ROWS, W, C)).astype(jnp.bfloat16)
    activated = jax.nn.silu(scaled_rms(mixed)).astype(jnp.bfloat16)
    padded = jnp.pad(activated.astype(jnp.float32), ((2, 0), (1, 1), (1, 1), (0, 0)))
    conv_sum = lax.conv_general_dilated(padded[None], conv_weight.astype(jnp.float32), (1, 1, 1), 'VALID', dimension_numbers=('NDHWC', 'DHWIO', 'NDHWC'), precision=lax.Precision.HIGHEST)[0]
    return (mixed.astype(jnp.float32) + conv_sum).astype(jnp.bfloat16)
```

```python
import math

import jax
import jax.numpy as jnp
from jax import lax
from jax.sharding import PartitionSpec as P

C = 384
W = 64
RD = 2
FD = 2


epsilon = 1e-06


def scaled_rms(values):
    wide = values.astype(jnp.float32)
    return wide / jnp.sqrt(jnp.mean(wide * wide, axis=-1, keepdims=True) + epsilon)


def attend(queries, key_rows, value_rows):
    scale = 1.0 / math.sqrt(queries.shape[-1])
    scores = (
        jnp.einsum("fqc,fkc->fqk", queries, key_rows, preferred_element_type=jnp.float32) * scale
    )
    largest = jnp.max(scores, axis=-1, keepdims=True)
    powers = jnp.exp(scores - largest)
    totals = jnp.sum(powers, axis=-1, keepdims=True)
    weights = powers.astype(jnp.bfloat16)
    summed = jnp.einsum("fqk,fkc->fqc", weights, value_rows, preferred_element_type=jnp.float32)
    return summed / totals


def spatial_conv(frames, kernel):
    return lax.conv_general_dilated(
        frames,
        kernel,
        (1, 1),
        ((0, 0), (1, 1)),
        dimension_numbers=("NHWC", "HWIO", "NHWC"),
        preferred_element_type=jnp.float32,
    )


def local(latent_tiles, route, w_query, w_keyval, conv_weight):
    patch_count = lax.axis_size("patch")
    patch_index = lax.axis_index("patch")
    chan_count = lax.axis_size("chan")
    chan_index = lax.axis_index("chan")
    span_count = lax.axis_size("span")
    table = route[0]
    block = latent_tiles.shape[1]
    share = block // chan_count
    own_share = lax.dynamic_slice_in_dim(latent_tiles, chan_index * share, share, 1)
    every_tile = lax.all_gather(own_share, ("patch", "chan"), axis=1, tiled=True)[0]
    tile_total = every_tile.shape[0]
    rows = patch_count * RD
    inverse = (
        jnp.zeros((tile_total,), jnp.int32).at[table].set(jnp.arange(tile_total, dtype=jnp.int32))
    )
    placed = jnp.take(every_tile, inverse, axis=0).reshape(patch_count, FD, RD, W, C)
    whole = placed.transpose(1, 0, 2, 3, 4).reshape(FD, rows, W, C)
    normed_all = scaled_rms(whole).astype(jnp.bfloat16)
    padded = jnp.pad(whole, ((0, 0), (1, 1), (0, 0), (0, 0)))
    features = lax.dynamic_slice_in_dim(padded, patch_index * RD, RD + 2, 1)
    normed = scaled_rms(features).astype(jnp.bfloat16)
    ext_cells = (RD + 2) * W
    queries = jnp.einsum(
        "fnc,cd->fnd", normed.reshape(FD, ext_cells, C), w_query, preferred_element_type=jnp.float32
    ).astype(jnp.bfloat16)
    keyvals = jnp.einsum(
        "fnc,cd->fnd",
        normed_all.reshape(FD, rows * W, C),
        w_keyval,
        preferred_element_type=jnp.float32,
    ).astype(jnp.bfloat16)
    attended = attend(queries, keyvals[..., :C], keyvals[..., C:])
    mixed = (features.astype(jnp.float32) + attended.reshape(FD, RD + 2, W, C)).astype(
        jnp.bfloat16
    )
    row_ids = patch_index * RD - 1 + jnp.arange(RD + 2)
    inside = ((row_ids >= 0) & (row_ids < rows))[None, :, None, None]
    activated = jnp.where(inside, jax.nn.silu(scaled_rms(mixed)), 0.0).astype(jnp.bfloat16)
    tap_sums = [spatial_conv(activated, conv_weight[a]) for a in range(3)]
    to_next = jnp.stack([tap_sums[0][0] + tap_sums[1][1], tap_sums[0][1]])
    pairs = [(i, i + 1) for i in range(span_count - 1)]
    from_prev = lax.ppermute(to_next, "span", pairs)
    own_sum = jnp.stack([tap_sums[2][0], tap_sums[1][0] + tap_sums[2][1]])
    out_width = conv_weight.shape[-1]
    own_rows = mixed[:, 1 : RD + 1]
    own_channels = lax.dynamic_slice_in_dim(own_rows, chan_index * out_width, out_width, 3)
    return (own_channels.astype(jnp.float32) + own_sum + from_prev).astype(jnp.bfloat16)


def solution(mesh):
    placed = (
        P(("clips", "span"), "patch", None, None),
        P(("clips", "span"), None),
        P(),
        P(),
        P(None, None, None, None, "chan"),
    )
    return jax.shard_map(
        local,
        mesh=mesh,
        in_specs=placed,
        out_specs=P(("clips", "span"), "patch", None, "chan"),
        check_vma=False,
    )
```

```python
import math

import jax
import jax.numpy as jnp
from jax import lax
from jax.sharding import PartitionSpec as P

C = 384
W = 64
RD = 2
FD = 2


epsilon = 1e-06


def scaled_rms(values):
    wide = values.astype(jnp.float32)
    return wide / jnp.sqrt(jnp.mean(wide * wide, axis=-1, keepdims=True) + epsilon)


def attend(queries, key_rows, value_rows):
    scale = 1.0 / math.sqrt(queries.shape[-1])
    scores = (
        jnp.einsum("fqc,fkc->fqk", queries, key_rows, preferred_element_type=jnp.float32) * scale
    )
    largest = jnp.max(scores, axis=-1, keepdims=True)
    powers = jnp.exp(scores - largest)
    totals = jnp.sum(powers, axis=-1, keepdims=True)
    weights = powers.astype(jnp.bfloat16)
    summed = jnp.einsum("fqk,fkc->fqc", weights, value_rows, preferred_element_type=jnp.float32)
    return summed / totals


def spatial_conv(frames, kernel):
    return lax.conv_general_dilated(
        frames,
        kernel,
        (1, 1),
        ((0, 0), (1, 1)),
        dimension_numbers=("NHWC", "HWIO", "NHWC"),
        preferred_element_type=jnp.float32,
    )


def local(latent_tiles, route, w_query, w_keyval, conv_weight):
    patch_count = lax.axis_size("patch")
    patch_index = lax.axis_index("patch")
    chan_count = lax.axis_size("chan")
    chan_index = lax.axis_index("chan")
    span_count = lax.axis_size("span")
    table = route[0]
    block = latent_tiles.shape[1]
    share = block // chan_count
    own_share = lax.dynamic_slice_in_dim(latent_tiles, chan_index * share, share, 1)
    every_tile = lax.all_gather(own_share, ("patch", "chan"), axis=1, tiled=True)[0]
    tile_total = every_tile.shape[0]
    rows = patch_count * RD
    slots = jnp.arange(tile_total, dtype=jnp.int32)
    one_hot = (slots[:, None] == table[None, :]).astype(jnp.bfloat16)
    placed = jnp.dot(
        one_hot, every_tile.reshape(tile_total, -1), preferred_element_type=jnp.float32
    ).astype(jnp.bfloat16)
    placed = placed.reshape(patch_count, FD, RD, W, C)
    whole = placed.transpose(1, 0, 2, 3, 4).reshape(FD, rows, W, C)
    normed_all = scaled_rms(whole).astype(jnp.bfloat16)
    padded = jnp.pad(whole, ((0, 0), (1, 1), (0, 0), (0, 0)))
    features = lax.dynamic_slice_in_dim(padded, patch_index * RD, RD + 2, 1)
    normed = scaled_rms(features).astype(jnp.bfloat16)
    ext_cells = (RD + 2) * W
    queries = jnp.einsum(
        "fnc,cd->fnd", normed.reshape(FD, ext_cells, C), w_query, preferred_element_type=jnp.float32
    ).astype(jnp.bfloat16)
    keyvals = jnp.einsum(
        "fnc,cd->fnd",
        normed_all.reshape(FD, rows * W, C),
        w_keyval,
        preferred_element_type=jnp.float32,
    ).astype(jnp.bfloat16)
    attended = attend(queries, keyvals[..., :C], keyvals[..., C:])
    mixed = (features.astype(jnp.float32) + attended.reshape(FD, RD + 2, W, C)).astype(
        jnp.bfloat16
    )
    row_ids = patch_index * RD - 1 + jnp.arange(RD + 2)
    inside = ((row_ids >= 0) & (row_ids < rows))[None, :, None, None]
    activated = jnp.where(inside, jax.nn.silu(scaled_rms(mixed)), 0.0).astype(jnp.bfloat16)
    tap_sums = [spatial_conv(activated, conv_weight[a]) for a in range(3)]
    to_next = jnp.stack([tap_sums[0][0] + tap_sums[1][1], tap_sums[0][1]]).astype(jnp.bfloat16)
    pairs = [(i, i + 1) for i in range(span_count - 1)]
    from_prev = lax.ppermute(to_next, "span", pairs)
    own_sum = jnp.stack([tap_sums[2][0], tap_sums[1][0] + tap_sums[2][1]])
    out_width = conv_weight.shape[-1]
    own_rows = mixed[:, 1 : RD + 1]
    own_channels = lax.dynamic_slice_in_dim(own_rows, chan_index * out_width, out_width, 3)
    return (own_channels.astype(jnp.float32) + own_sum + from_prev.astype(jnp.float32)).astype(jnp.bfloat16)


def solution(mesh):
    placed = (
        P(("clips", "span"), "patch", None, None),
        P(("clips", "span"), None),
        P(),
        P(),
        P(None, None, None, None, "chan"),
    )
    return jax.shard_map(
        local,
        mesh=mesh,
        in_specs=placed,
        out_specs=P(("clips", "span"), "patch", None, "chan"),
        check_vma=False,
    )
```

```python
import functools
import math

import jax
import jax.numpy as jnp
from jax import lax
from jax.experimental import pallas as pl
from jax.sharding import PartitionSpec as P

C = 384
W = 64
RD = 2
FD = 2
KEY_BLOCK = 512


epsilon = 1e-06


def scaled_rms(values):
    wide = values.astype(jnp.float32)
    return wide / jnp.sqrt(jnp.mean(wide * wide, axis=-1, keepdims=True) + epsilon)


def attention_kernel(cells_ref, query_ref, mask_ref, wq_ref, wkv_ref, mixed_ref, act_ref):
    width = wq_ref.shape[0]
    scale = 1.0 / math.sqrt(width)
    feats = query_ref[0].astype(jnp.float32)
    queries = jnp.dot(
        scaled_rms(feats).astype(jnp.bfloat16), wq_ref[...], preferred_element_type=jnp.float32
    ).astype(jnp.bfloat16)
    count = cells_ref.shape[1]
    block = min(count, KEY_BLOCK)

    def fold(step, carry):
        run_max, run_total, run_acc = carry
        cells = cells_ref[0, pl.ds(step * block, block), :]
        keyvals = jnp.dot(
            scaled_rms(cells).astype(jnp.bfloat16), wkv_ref[...], preferred_element_type=jnp.float32
        ).astype(jnp.bfloat16)
        scores = (
            lax.dot_general(
                queries,
                keyvals[:, :width],
                (((1,), (1,)), ((), ())),
                preferred_element_type=jnp.float32,
            )
            * scale
        )
        new_max = jnp.maximum(run_max, jnp.max(scores, axis=-1, keepdims=True))
        factor = jnp.exp(run_max - new_max)
        powers = jnp.exp(scores - new_max)
        run_total = run_total * factor + jnp.sum(powers, axis=-1, keepdims=True)
        run_acc = run_acc * factor + jnp.dot(
            powers.astype(jnp.bfloat16), keyvals[:, width:], preferred_element_type=jnp.float32
        )
        return new_max, run_total, run_acc

    rows = feats.shape[0]
    carry = (
        jnp.full((rows, 1), -jnp.inf, jnp.float32),
        jnp.zeros((rows, 1), jnp.float32),
        jnp.zeros((rows, width), jnp.float32),
    )
    steps = count // block
    if steps == 1:
        carry = fold(0, carry)
    else:
        carry = lax.fori_loop(0, steps, fold, carry)
    _, run_total, run_acc = carry
    mixed = (feats + run_acc / run_total).astype(jnp.bfloat16)
    mixed_ref[0] = mixed
    normed = scaled_rms(mixed)
    act_ref[0] = (normed / (1.0 + jnp.exp(-normed)) * mask_ref[...]).astype(jnp.bfloat16)


def attend_frames(cells, query_feats, mask, w_query, w_keyval):
    frames, count, width = cells.shape
    rows = query_feats.shape[1]
    out = jax.ShapeDtypeStruct((frames, rows, width), jnp.bfloat16)
    return pl.pallas_call(
        attention_kernel,
        grid=(frames,),
        in_specs=[
            pl.BlockSpec((1, count, width), lambda f: (f, 0, 0)),
            pl.BlockSpec((1, rows, width), lambda f: (f, 0, 0)),
            pl.BlockSpec((rows, 1), lambda f: (0, 0)),
            pl.BlockSpec(w_query.shape, lambda f: (0, 0)),
            pl.BlockSpec(w_keyval.shape, lambda f: (0, 0)),
        ],
        out_specs=[
            pl.BlockSpec((1, rows, width), lambda f: (f, 0, 0)),
            pl.BlockSpec((1, rows, width), lambda f: (f, 0, 0)),
        ],
        out_shape=[out, out],
    )(cells, query_feats, mask, w_query, w_keyval)


def spatial_conv(frames, kernel):
    return lax.conv_general_dilated(
        frames,
        kernel,
        (1, 1),
        ((0, 0), (1, 1)),
        dimension_numbers=("NHWC", "HWIO", "NHWC"),
        preferred_element_type=jnp.float32,
    )


def local(latent_tiles, route, w_query, w_keyval, conv_weight):
    patch_count = lax.axis_size("patch")
    patch_index = lax.axis_index("patch")
    chan_count = lax.axis_size("chan")
    chan_index = lax.axis_index("chan")
    span_count = lax.axis_size("span")
    table = route[0]
    block = latent_tiles.shape[1]
    share = block // chan_count
    own_share = lax.dynamic_slice_in_dim(latent_tiles, chan_index * share, share, 1)
    every_tile = lax.all_gather(own_share, ("patch", "chan"), axis=1, tiled=True)[0]
    tile_total = every_tile.shape[0]
    rows = patch_count * RD
    per_owner = tile_total // patch_count
    per_frame = per_owner // FD
    owner = table // per_owner
    spot = table % per_owner
    dest = (spot // per_frame) * (tile_total // FD) + owner * per_frame + spot % per_frame
    slots = jnp.arange(tile_total, dtype=jnp.int32)
    one_hot = (slots[:, None] == dest[None, :]).astype(jnp.bfloat16)
    placed = jnp.dot(
        one_hot, every_tile.reshape(tile_total, -1), preferred_element_type=jnp.float32
    ).astype(jnp.bfloat16)
    whole = placed.reshape(FD, rows, W, C)
    padded = jnp.pad(whole, ((0, 0), (1, 1), (0, 0), (0, 0)))
    features = lax.dynamic_slice_in_dim(padded, patch_index * RD, RD + 2, 1)
    ext_cells = (RD + 2) * W
    row_ids = patch_index * RD - 1 + jnp.arange(RD + 2)
    inside = ((row_ids >= 0) & (row_ids < rows)).astype(jnp.float32)
    mask = jnp.repeat(inside, W)[:, None]
    mixed, activated = attend_frames(
        whole.reshape(FD, rows * W, C),
        features.reshape(FD, ext_cells, C),
        mask,
        w_query,
        w_keyval,
    )
    mixed = mixed.reshape(FD, RD + 2, W, C)
    activated = activated.reshape(FD, RD + 2, W, C)
    tap_sums = [spatial_conv(activated, conv_weight[a]) for a in range(3)]
    to_next = jnp.stack([tap_sums[0][0] + tap_sums[1][1], tap_sums[0][1]]).astype(jnp.bfloat16)
    pairs = [(i, i + 1) for i in range(span_count - 1)]
    from_prev = lax.ppermute(to_next, "span", pairs)
    own_sum = jnp.stack([tap_sums[2][0], tap_sums[1][0] + tap_sums[2][1]])
    out_width = conv_weight.shape[-1]
    own_rows = mixed[:, 1 : RD + 1]
    own_channels = lax.dynamic_slice_in_dim(own_rows, chan_index * out_width, out_width, 3)
    total = own_channels.astype(jnp.float32) + own_sum + from_prev.astype(jnp.float32)
    return total.astype(jnp.bfloat16)


def solution(mesh):
    placed = (
        P(("clips", "span"), "patch", None, None),
        P(("clips", "span"), None),
        P(),
        P(),
        P(None, None, None, None, "chan"),
    )
    return jax.shard_map(
        local,
        mesh=mesh,
        in_specs=placed,
        out_specs=P(("clips", "span"), "patch", None, "chan"),
        check_vma=False,
    )
```

```python
import math

import jax
import jax.numpy as jnp
from jax import lax
from jax.experimental import pallas as pl
from jax.sharding import PartitionSpec as P

C = 384
W = 64
RD = 2
FD = 2
KEY_BLOCK = 512


epsilon = 1e-06


def scaled_rms(values):
    wide = values.astype(jnp.float32)
    return wide / jnp.sqrt(jnp.mean(wide * wide, axis=-1, keepdims=True) + epsilon)


def attend_frame(cells_ref, frame, feats, wq_ref, wkv_ref):
    width = wq_ref.shape[0]
    scale = 1.0 / math.sqrt(width)
    queries = jnp.dot(
        scaled_rms(feats).astype(jnp.bfloat16), wq_ref[...], preferred_element_type=jnp.float32
    ).astype(jnp.bfloat16)
    count = cells_ref.shape[1]
    block = min(count, KEY_BLOCK)

    def fold(step, carry):
        run_max, run_total, run_acc = carry
        cells = cells_ref[frame, pl.ds(step * block, block), :]
        keyvals = jnp.dot(
            scaled_rms(cells).astype(jnp.bfloat16), wkv_ref[...], preferred_element_type=jnp.float32
        ).astype(jnp.bfloat16)
        scores = (
            lax.dot_general(
                queries,
                keyvals[:, :width],
                (((1,), (1,)), ((), ())),
                preferred_element_type=jnp.float32,
            )
            * scale
        )
        new_max = jnp.maximum(run_max, jnp.max(scores, axis=-1, keepdims=True))
        factor = jnp.exp(run_max - new_max)
        powers = jnp.exp(scores - new_max)
        run_total = run_total * factor + jnp.sum(powers, axis=-1, keepdims=True)
        run_acc = run_acc * factor + jnp.dot(
            powers.astype(jnp.bfloat16), keyvals[:, width:], preferred_element_type=jnp.float32
        )
        return new_max, run_total, run_acc

    rows = feats.shape[0]
    carry = (
        jnp.full((rows, 1), -jnp.inf, jnp.float32),
        jnp.zeros((rows, 1), jnp.float32),
        jnp.zeros((rows, width), jnp.float32),
    )
    for step in range(count // block):
        carry = fold(step, carry)
    _, run_total, run_acc = carry
    return (feats + run_acc / run_total).astype(jnp.bfloat16)


def block_kernel(
    cells_ref, query_ref, mask_ref, wq_ref, wkv_ref, conv_ref, mixed_ref, own_ref, next_ref
):
    frames, rows, width = query_ref.shape
    out_rows = mixed_ref.shape[1]
    taps = conv_ref.shape[0]
    line = (rows - out_rows) // 2
    place = lax.broadcasted_iota(jnp.int32, (rows, rows), 0)
    source = lax.broadcasted_iota(jnp.int32, (rows, rows), 1)
    column = place % line
    shifts = []
    for c in range(taps):
        offset = c - 1
        keep = (source == place + offset) & (column + offset >= 0) & (column + offset < line)
        shifts.append(keep.astype(jnp.bfloat16))
    own_acc = [None] * frames
    next_acc = [None] * frames

    def add(acc, index, value):
        acc[index] = value if acc[index] is None else acc[index] + value

    for f in range(frames):
        feats = query_ref[f].astype(jnp.float32)
        mixed = attend_frame(cells_ref, f, feats, wq_ref, wkv_ref)
        mixed_ref[f] = mixed[line : line + out_rows]
        normed = scaled_rms(mixed)
        activated = (normed / (1.0 + jnp.exp(-normed)) * mask_ref[...]).astype(jnp.bfloat16)
        moved = [
            jnp.dot(shifts[c], activated, preferred_element_type=jnp.float32).astype(jnp.bfloat16)
            for c in range(taps)
        ]
        for b in range(taps):
            for c in range(taps):
                window = moved[c][b * line : b * line + out_rows]
                for t in range(frames):
                    a = f + taps - 1 - t
                    if 0 <= a < taps:
                        add(own_acc, t, jnp.dot(window, conv_ref[a, b, c], preferred_element_type=jnp.float32))
                    a = f - t
                    if 0 <= a < taps:
                        add(next_acc, t, jnp.dot(window, conv_ref[a, b, c], preferred_element_type=jnp.float32))
    for t in range(frames):
        own_ref[t] = own_acc[t]
        next_ref[t] = next_acc[t].astype(next_ref.dtype)


def fused_block(cells, query_feats, mask, w_query, w_keyval, conv_weight):
    frames, count, width = cells.shape
    rows = query_feats.shape[1]
    out_rows = RD * (rows // (RD + 2))
    out_width = conv_weight.shape[-1]

    def whole(shape):
        return pl.BlockSpec(shape, lambda i: (0,) * len(shape))

    return pl.pallas_call(
        block_kernel,
        grid=(1,),
        in_specs=[
            whole(cells.shape),
            whole(query_feats.shape),
            whole(mask.shape),
            whole(w_query.shape),
            whole(w_keyval.shape),
            whole(conv_weight.shape),
        ],
        out_specs=[
            whole((frames, out_rows, width)),
            whole((frames, out_rows, out_width)),
            whole((frames, out_rows, out_width)),
        ],
        out_shape=[
            jax.ShapeDtypeStruct((frames, out_rows, width), jnp.bfloat16),
            jax.ShapeDtypeStruct((frames, out_rows, out_width), jnp.float32),
            jax.ShapeDtypeStruct((frames, out_rows, out_width), jnp.bfloat16),
        ],
    )(cells, query_feats, mask, w_query, w_keyval, conv_weight)


def local(latent_tiles, route, w_query, w_keyval, conv_weight):
    patch_count = lax.axis_size("patch")
    patch_index = lax.axis_index("patch")
    chan_count = lax.axis_size("chan")
    chan_index = lax.axis_index("chan")
    span_count = lax.axis_size("span")
    table = route[0]
    block = latent_tiles.shape[1]
    share = block // chan_count
    own_share = lax.dynamic_slice_in_dim(latent_tiles, chan_index * share, share, 1)
    every_tile = lax.all_gather(own_share, ("patch", "chan"), axis=1, tiled=True)[0]
    tile_total = every_tile.shape[0]
    rows = patch_count * RD
    per_owner = tile_total // patch_count
    per_frame = per_owner // FD
    owner = table // per_owner
    spot = table % per_owner
    dest = (spot // per_frame) * (tile_total // FD) + owner * per_frame + spot % per_frame
    slots = jnp.arange(tile_total, dtype=jnp.int32)
    one_hot = (slots[:, None] == dest[None, :]).astype(jnp.bfloat16)
    placed = jnp.dot(
        one_hot, every_tile.reshape(tile_total, -1), preferred_element_type=jnp.float32
    ).astype(jnp.bfloat16)
    whole = placed.reshape(FD, rows, W, C)
    padded = jnp.pad(whole, ((0, 0), (1, 1), (0, 0), (0, 0)))
    features = lax.dynamic_slice_in_dim(padded, patch_index * RD, RD + 2, 1)
    ext_cells = (RD + 2) * W
    row_ids = patch_index * RD - 1 + jnp.arange(RD + 2)
    inside = ((row_ids >= 0) & (row_ids < rows)).astype(jnp.float32)
    mask = jnp.repeat(inside, W)[:, None]
    mixed_own, own_sum, to_next = fused_block(
        whole.reshape(FD, rows * W, C),
        features.reshape(FD, ext_cells, C),
        mask,
        w_query,
        w_keyval,
        conv_weight,
    )
    pairs = [(i, i + 1) for i in range(span_count - 1)]
    from_prev = lax.ppermute(to_next, "span", pairs)
    out_width = conv_weight.shape[-1]
    own_channels = lax.dynamic_slice_in_dim(mixed_own, chan_index * out_width, out_width, 2)
    total = own_channels.astype(jnp.float32) + own_sum + from_prev.astype(jnp.float32)
    return total.reshape(FD, RD, W, out_width).astype(jnp.bfloat16)


def solution(mesh):
    placed = (
        P(("clips", "span"), "patch", None, None),
        P(("clips", "span"), None),
        P(),
        P(),
        P(None, None, None, None, "chan"),
    )
    return jax.shard_map(
        local,
        mesh=mesh,
        in_specs=placed,
        out_specs=P(("clips", "span"), "patch", None, "chan"),
        check_vma=False,
    )
```

```python
import math

import jax
import jax.numpy as jnp
from jax import lax
from jax.experimental import pallas as pl
from jax.experimental.pallas import tpu as pltpu
from jax.sharding import PartitionSpec as P

C = 384
W = 64
RD = 2
FD = 2
KEY_BLOCK = 512


epsilon = 1e-06


def scaled_rms(values):
    wide = values.astype(jnp.float32)
    return wide / jnp.sqrt(jnp.mean(wide * wide, axis=-1, keepdims=True) + epsilon)


def attend_frame(cells_ref, frame, feats, wq_ref, wkv_ref):
    width = wq_ref.shape[0]
    scale = 1.0 / math.sqrt(width)
    queries = jnp.dot(
        scaled_rms(feats).astype(jnp.bfloat16), wq_ref[...], preferred_element_type=jnp.float32
    ).astype(jnp.bfloat16)
    count = cells_ref.shape[1]
    block = min(count, KEY_BLOCK)

    def fold(step, carry):
        run_max, run_total, run_acc = carry
        cells = cells_ref[frame, pl.ds(step * block, block), :]
        keyvals = jnp.dot(
            scaled_rms(cells).astype(jnp.bfloat16), wkv_ref[...], preferred_element_type=jnp.float32
        ).astype(jnp.bfloat16)
        scores = (
            lax.dot_general(
                queries,
                keyvals[:, :width],
                (((1,), (1,)), ((), ())),
                preferred_element_type=jnp.float32,
            )
            * scale
        )
        new_max = jnp.maximum(run_max, jnp.max(scores, axis=-1, keepdims=True))
        factor = jnp.exp(run_max - new_max)
        powers = jnp.exp(scores - new_max)
        run_total = run_total * factor + jnp.sum(powers, axis=-1, keepdims=True)
        run_acc = run_acc * factor + jnp.dot(
            powers.astype(jnp.bfloat16), keyvals[:, width:], preferred_element_type=jnp.float32
        )
        return new_max, run_total, run_acc

    rows = feats.shape[0]
    carry = (
        jnp.full((rows, 1), -jnp.inf, jnp.float32),
        jnp.zeros((rows, 1), jnp.float32),
        jnp.zeros((rows, width), jnp.float32),
    )
    for step in range(count // block):
        carry = fold(step, carry)
    _, run_total, run_acc = carry
    return (feats + run_acc / run_total).astype(jnp.bfloat16)


def block_kernel(
    first_ref, cells_ref, query_ref, wq_ref, wkv_ref, conv_ref, mixed_ref, own_ref, next_ref
):
    frames, rows, width = query_ref.shape
    out_rows = mixed_ref.shape[1]
    taps = conv_ref.shape[0]
    line = (rows - out_rows) // 2
    frame_rows = cells_ref.shape[1] // line
    place = lax.broadcasted_iota(jnp.int32, (rows, rows), 0)
    source = lax.broadcasted_iota(jnp.int32, (rows, rows), 1)
    column = place % line
    shifts = []
    for c in range(taps):
        offset = c - 1
        keep = (source == place + offset) & (column + offset >= 0) & (column + offset < line)
        shifts.append(keep.astype(jnp.bfloat16))
    row_of = lax.broadcasted_iota(jnp.int32, (rows, width), 0) // line + first_ref[0]
    inside = (row_of >= 0) & (row_of < frame_rows)
    moved = []
    for f in range(frames):
        feats = query_ref[f].astype(jnp.float32)
        mixed = attend_frame(cells_ref, f, feats, wq_ref, wkv_ref)
        mixed_ref[f] = mixed[line : line + out_rows]
        normed = scaled_rms(mixed)
        activated = jnp.where(inside, normed / (1.0 + jnp.exp(-normed)), 0.0).astype(jnp.bfloat16)
        moved.append(
            [
                jnp.dot(shifts[c], activated, preferred_element_type=jnp.float32).astype(
                    jnp.bfloat16
                )
                for c in range(taps)
            ]
        )
    own_acc = [None] * frames
    next_acc = [None] * frames
    for a in range(taps):
        targets = []
        for f in range(frames):
            if 0 <= f + taps - 1 - a < frames:
                targets.append((f, own_acc, f + taps - 1 - a))
            if 0 <= f - a < frames:
                targets.append((f, next_acc, f - a))
        total = None
        for b in range(taps):
            for c in range(taps):
                window = jnp.concatenate(
                    [moved[f][c][b * line : b * line + out_rows] for f, _, _ in targets], axis=0
                )
                part = lax.dot_general(
                    window,
                    conv_ref[a, b, c],
                    (((1,), (1,)), ((), ())),
                    preferred_element_type=jnp.float32,
                )
                total = part if total is None else total + part
        for k, (_, acc, t) in enumerate(targets):
            piece = total[k * out_rows : (k + 1) * out_rows]
            acc[t] = piece if acc[t] is None else acc[t] + piece
    for t in range(frames):
        own_ref[t] = own_acc[t]
        next_ref[t] = next_acc[t].astype(next_ref.dtype)


def fused_block(first, cells, query_feats, w_query, w_keyval, conv_weight):
    frames, count, width = cells.shape
    rows = query_feats.shape[1]
    out_rows = RD * (rows // (RD + 2))
    out_width = conv_weight.shape[-1]
    flipped = jnp.swapaxes(conv_weight, 3, 4)

    def whole(shape):
        return pl.BlockSpec(shape, lambda i, first_ref: (0,) * len(shape))

    grid_spec = pltpu.PrefetchScalarGridSpec(
        num_scalar_prefetch=1,
        grid=(1,),
        in_specs=[
            whole(cells.shape),
            whole(query_feats.shape),
            whole(w_query.shape),
            whole(w_keyval.shape),
            whole(flipped.shape),
        ],
        out_specs=[
            whole((frames, out_rows, width)),
            whole((frames, out_rows, out_width)),
            whole((frames, out_rows, out_width)),
        ],
    )
    return pl.pallas_call(
        block_kernel,
        grid_spec=grid_spec,
        out_shape=[
            jax.ShapeDtypeStruct((frames, out_rows, width), jnp.bfloat16),
            jax.ShapeDtypeStruct((frames, out_rows, out_width), jnp.float32),
            jax.ShapeDtypeStruct((frames, out_rows, out_width), jnp.bfloat16),
        ],
    )(first, cells, query_feats, w_query, w_keyval, flipped)


def local(latent_tiles, route, w_query, w_keyval, conv_weight):
    patch_count = lax.axis_size("patch")
    patch_index = lax.axis_index("patch")
    chan_count = lax.axis_size("chan")
    chan_index = lax.axis_index("chan")
    span_count = lax.axis_size("span")
    table = route[0]
    block = latent_tiles.shape[1]
    share = block // chan_count
    own_share = lax.dynamic_slice_in_dim(latent_tiles, chan_index * share, share, 1)
    every_tile = lax.all_gather(own_share, ("patch", "chan"), axis=1, tiled=True)[0]
    tile_total = every_tile.shape[0]
    rows = patch_count * RD
    per_owner = tile_total // patch_count
    per_frame = per_owner // FD
    owner = table // per_owner
    spot = table % per_owner
    dest = (spot // per_frame) * (tile_total // FD) + owner * per_frame + spot % per_frame
    slots = jnp.arange(tile_total, dtype=jnp.int32)
    one_hot = (slots[:, None] == dest[None, :]).astype(jnp.bfloat16)
    placed = jnp.dot(
        one_hot, every_tile.reshape(tile_total, -1), preferred_element_type=jnp.float32
    ).astype(jnp.bfloat16)
    whole = placed.reshape(FD, rows, W, C)
    padded = jnp.pad(whole, ((0, 0), (1, 1), (0, 0), (0, 0)))
    features = lax.dynamic_slice_in_dim(padded, patch_index * RD, RD + 2, 1)
    ext_cells = (RD + 2) * W
    first = jnp.reshape(patch_index * RD - 1, (1,)).astype(jnp.int32)
    mixed_own, own_sum, to_next = fused_block(
        first,
        whole.reshape(FD, rows * W, C),
        features.reshape(FD, ext_cells, C),
        w_query,
        w_keyval,
        conv_weight,
    )
    pairs = [(i, i + 1) for i in range(span_count - 1)]
    from_prev = lax.ppermute(to_next, "span", pairs)
    out_width = conv_weight.shape[-1]
    own_channels = lax.dynamic_slice_in_dim(mixed_own, chan_index * out_width, out_width, 2)
    total = own_channels.astype(jnp.float32) + own_sum + from_prev.astype(jnp.float32)
    return total.reshape(FD, RD, W, out_width).astype(jnp.bfloat16)


def solution(mesh):
    placed = (
        P(("clips", "span"), "patch", None, None),
        P(("clips", "span"), None),
        P(),
        P(),
        P(None, None, None, None, "chan"),
    )
    return jax.shard_map(
        local,
        mesh=mesh,
        in_specs=placed,
        out_specs=P(("clips", "span"), "patch", None, "chan"),
        check_vma=False,
    )
```

```python
import math

import jax
import jax.numpy as jnp
from jax import lax
from jax.sharding import PartitionSpec as P

C = 384
W = 64
RD = 2
FD = 2


epsilon = 1e-06


def scaled_rms(values):
    wide = values.astype(jnp.float32)
    return wide / jnp.sqrt(jnp.mean(wide * wide, axis=-1, keepdims=True) + epsilon)


def attend(queries, key_rows, value_rows):
    scale = 1.0 / math.sqrt(queries.shape[-1])
    scores = (
        jnp.einsum("fqc,fkc->fqk", queries, key_rows, preferred_element_type=jnp.float32) * scale
    )
    largest = jnp.max(scores, axis=-1, keepdims=True)
    powers = jnp.exp(scores - largest)
    totals = jnp.sum(powers, axis=-1, keepdims=True)
    weights = powers.astype(jnp.bfloat16)
    summed = jnp.einsum("fqk,fkc->fqc", weights, value_rows, preferred_element_type=jnp.float32)
    return summed / totals


def spatial_conv(frames, kernel):
    return lax.conv_general_dilated(
        frames,
        kernel,
        (1, 1),
        ((0, 0), (1, 1)),
        dimension_numbers=("NHWC", "HWIO", "NHWC"),
        preferred_element_type=jnp.float32,
    )


def local(latent_tiles, route, w_query, w_keyval, conv_weight):
    patch_count = lax.axis_size("patch")
    patch_index = lax.axis_index("patch")
    chan_count = lax.axis_size("chan")
    chan_index = lax.axis_index("chan")
    span_count = lax.axis_size("span")
    table = route[0]
    block = latent_tiles.shape[1]
    share = block // chan_count
    own_share = lax.dynamic_slice_in_dim(latent_tiles, chan_index * share, share, 1)
    every_tile = lax.all_gather(own_share, ("patch", "chan"), axis=1, tiled=True)[0]
    tile_total = every_tile.shape[0]
    rows = patch_count * RD
    slots = jnp.arange(tile_total, dtype=jnp.int32)
    one_hot = (slots[:, None] == table[None, :]).astype(jnp.bfloat16)
    placed = jnp.dot(
        one_hot, every_tile.reshape(tile_total, -1), preferred_element_type=jnp.float32
    ).astype(jnp.bfloat16)
    placed = placed.reshape(patch_count, FD, RD, W, C)
    whole = placed.transpose(1, 0, 2, 3, 4).reshape(FD, rows, W, C)
    normed_all = scaled_rms(whole).astype(jnp.bfloat16)
    padded = jnp.pad(whole, ((0, 0), (1, 1), (0, 0), (0, 0)))
    features = lax.dynamic_slice_in_dim(padded, patch_index * RD, RD + 2, 1)
    normed = scaled_rms(features).astype(jnp.bfloat16)
    ext_cells = (RD + 2) * W
    queries = jnp.einsum(
        "fnc,cd->fnd", normed.reshape(FD, ext_cells, C), w_query, preferred_element_type=jnp.float32
    ).astype(jnp.bfloat16)
    keyvals = jnp.einsum(
        "fnc,cd->fnd",
        normed_all.reshape(FD, rows * W, C),
        w_keyval,
        preferred_element_type=jnp.float32,
    ).astype(jnp.bfloat16)
    attended = attend(queries, keyvals[..., :C], keyvals[..., C:])
    mixed = (features.astype(jnp.float32) + attended.reshape(FD, RD + 2, W, C)).astype(
        jnp.bfloat16
    )
    row_ids = patch_index * RD - 1 + jnp.arange(RD + 2)
    inside = ((row_ids >= 0) & (row_ids < rows))[None, :, None, None]
    activated = jnp.where(inside, jax.nn.silu(scaled_rms(mixed)), 0.0).astype(jnp.bfloat16)
    by_first = spatial_conv(activated, conv_weight[0])
    by_middle = spatial_conv(activated[1:], conv_weight[1])
    to_next = jnp.concatenate([by_first[:1] + by_middle, by_first[1:]]).astype(jnp.bfloat16)
    pairs = [(i, i + 1) for i in range(span_count - 1)]
    from_prev = lax.ppermute(to_next, "span", pairs)
    by_last = spatial_conv(activated, conv_weight[2])
    own_middle = spatial_conv(activated[:1], conv_weight[1])
    own_sum = jnp.concatenate([by_last[:1], own_middle + by_last[1:]])
    out_width = conv_weight.shape[-1]
    own_rows = mixed[:, 1 : RD + 1]
    own_channels = lax.dynamic_slice_in_dim(own_rows, chan_index * out_width, out_width, 3)
    return (own_channels.astype(jnp.float32) + own_sum + from_prev.astype(jnp.float32)).astype(jnp.bfloat16)


def solution(mesh):
    placed = (
        P(("clips", "span"), "patch", None, None),
        P(("clips", "span"), None),
        P(),
        P(),
        P(None, None, None, None, "chan"),
    )
    return jax.shard_map(
        local,
        mesh=mesh,
        in_specs=placed,
        out_specs=P(("clips", "span"), "patch", None, "chan"),
        check_vma=False,
    )
```

```python
import math

import jax
import jax.numpy as jnp
from jax import lax
from jax.experimental import pallas as pl
from jax.experimental.pallas import tpu as pltpu
from jax.sharding import PartitionSpec as P

C = 384
W = 64
RD = 2
FD = 2
KEY_BLOCK = 512


epsilon = 1e-06


def scaled_rms(values):
    wide = values.astype(jnp.float32)
    return wide / jnp.sqrt(jnp.mean(wide * wide, axis=-1, keepdims=True) + epsilon)


def attention_kernel(first_ref, cells_ref, wq_ref, wkv_ref, mixed_ref, act_ref):
    width = wq_ref.shape[0]
    scale = 1.0 / math.sqrt(width)
    count = cells_ref.shape[1]
    own = mixed_ref.shape[1]
    line = (act_ref.shape[1] - own) // 2
    frame_rows = count // line
    first = first_ref[0]
    top = jnp.maximum(first, 0) * line
    below = jnp.minimum(first + 1 + own // line, frame_rows - 1) * line
    feats = jnp.concatenate(
        [
            cells_ref[0, pl.ds(top, line), :],
            cells_ref[0, pl.ds((first + 1) * line, own), :],
            cells_ref[0, pl.ds(below, line), :],
        ],
        axis=0,
    ).astype(jnp.float32)
    queries = jnp.dot(
        scaled_rms(feats).astype(jnp.bfloat16), wq_ref[...], preferred_element_type=jnp.float32
    ).astype(jnp.bfloat16)
    block = min(count, KEY_BLOCK)

    def fold(step, carry):
        run_max, run_total, run_acc = carry
        cells = cells_ref[0, pl.ds(step * block, block), :]
        keyvals = jnp.dot(
            scaled_rms(cells).astype(jnp.bfloat16), wkv_ref[...], preferred_element_type=jnp.float32
        ).astype(jnp.bfloat16)
        scores = (
            lax.dot_general(
                queries,
                keyvals[:, :width],
                (((1,), (1,)), ((), ())),
                preferred_element_type=jnp.float32,
            )
            * scale
        )
        new_max = jnp.maximum(run_max, jnp.max(scores, axis=-1, keepdims=True))
        factor = jnp.exp(run_max - new_max)
        powers = jnp.exp(scores - new_max)
        run_total = run_total * factor + jnp.sum(powers, axis=-1, keepdims=True)
        run_acc = run_acc * factor + jnp.dot(
            powers.astype(jnp.bfloat16), keyvals[:, width:], preferred_element_type=jnp.float32
        )
        return new_max, run_total, run_acc

    rows = feats.shape[0]
    carry = (
        jnp.full((rows, 1), -jnp.inf, jnp.float32),
        jnp.zeros((rows, 1), jnp.float32),
        jnp.zeros((rows, width), jnp.float32),
    )
    for step in range(count // block):
        carry = fold(step, carry)
    _, run_total, run_acc = carry
    mixed = (feats + run_acc / run_total).astype(jnp.bfloat16)
    mixed_ref[0] = mixed[line : line + own]
    normed = scaled_rms(mixed)
    row_of = lax.broadcasted_iota(jnp.int32, (rows, width), 0) // line + first
    inside = (row_of >= 0) & (row_of < frame_rows)
    act_ref[0] = jnp.where(inside, normed / (1.0 + jnp.exp(-normed)), 0.0).astype(jnp.bfloat16)


def attend_frames(first, cells, ext_rows, w_query, w_keyval):
    frames, count, width = cells.shape
    own = ext_rows - 2 * (ext_rows // (RD + 2))
    fixed = lambda f, first_ref: (0, 0)
    per_frame = lambda f, first_ref: (f, 0, 0)
    grid_spec = pltpu.PrefetchScalarGridSpec(
        num_scalar_prefetch=1,
        grid=(frames,),
        in_specs=[
            pl.BlockSpec((1, count, width), per_frame),
            pl.BlockSpec(w_query.shape, fixed),
            pl.BlockSpec(w_keyval.shape, fixed),
        ],
        out_specs=[
            pl.BlockSpec((1, own, width), per_frame),
            pl.BlockSpec((1, ext_rows, width), per_frame),
        ],
    )
    return pl.pallas_call(
        attention_kernel,
        grid_spec=grid_spec,
        out_shape=[
            jax.ShapeDtypeStruct((frames, own, width), jnp.bfloat16),
            jax.ShapeDtypeStruct((frames, ext_rows, width), jnp.bfloat16),
        ],
    )(first, cells, w_query, w_keyval)


def spatial_conv(frames, kernel):
    return lax.conv_general_dilated(
        frames,
        kernel,
        (1, 1),
        ((0, 0), (1, 1)),
        dimension_numbers=("NHWC", "HWIO", "NHWC"),
        preferred_element_type=jnp.float32,
    )


def local(latent_tiles, route, w_query, w_keyval, conv_weight):
    patch_count = lax.axis_size("patch")
    patch_index = lax.axis_index("patch")
    chan_count = lax.axis_size("chan")
    chan_index = lax.axis_index("chan")
    span_count = lax.axis_size("span")
    table = route[0]
    block = latent_tiles.shape[1]
    share = block // chan_count
    own_share = lax.dynamic_slice_in_dim(latent_tiles, chan_index * share, share, 1)
    every_tile = lax.all_gather(own_share, ("patch", "chan"), axis=1, tiled=True)[0]
    tile_total = every_tile.shape[0]
    rows = patch_count * RD
    per_owner = tile_total // patch_count
    per_frame = per_owner // FD
    owner = table // per_owner
    spot = table % per_owner
    dest = (spot // per_frame) * (tile_total // FD) + owner * per_frame + spot % per_frame
    slots = jnp.arange(tile_total, dtype=jnp.int32)
    one_hot = (slots[:, None] == dest[None, :]).astype(jnp.bfloat16)
    placed = jnp.dot(
        one_hot, every_tile.reshape(tile_total, -1), preferred_element_type=jnp.float32
    ).astype(jnp.bfloat16)
    whole = placed.reshape(FD, rows, W, C)
    first = jnp.reshape(patch_index * RD - 1, (1,)).astype(jnp.int32)
    mixed_own, activated = attend_frames(
        first, whole.reshape(FD, rows * W, C), (RD + 2) * W, w_query, w_keyval
    )
    activated = activated.reshape(FD, RD + 2, W, C)
    by_first = spatial_conv(activated, conv_weight[0])
    by_middle = spatial_conv(activated[1:], conv_weight[1])
    to_next = jnp.concatenate([by_first[:1] + by_middle, by_first[1:]]).astype(jnp.bfloat16)
    pairs = [(i, i + 1) for i in range(span_count - 1)]
    from_prev = lax.ppermute(to_next, "span", pairs)
    by_last = spatial_conv(activated, conv_weight[2])
    own_middle = spatial_conv(activated[:1], conv_weight[1])
    own_sum = jnp.concatenate([by_last[:1], own_middle + by_last[1:]])
    out_width = conv_weight.shape[-1]
    own_rows = mixed_own.reshape(FD, RD, W, C)
    own_channels = lax.dynamic_slice_in_dim(own_rows, chan_index * out_width, out_width, 3)
    total = own_channels.astype(jnp.float32) + own_sum + from_prev.astype(jnp.float32)
    return total.astype(jnp.bfloat16)


def solution(mesh):
    placed = (
        P(("clips", "span"), "patch", None, None),
        P(("clips", "span"), None),
        P(),
        P(),
        P(None, None, None, None, "chan"),
    )
    return jax.shard_map(
        local,
        mesh=mesh,
        in_specs=placed,
        out_specs=P(("clips", "span"), "patch", None, "chan"),
        check_vma=False,
    )
```

```python
import math

import jax
import jax.numpy as jnp
from jax import lax
from jax.experimental import pallas as pl
from jax.experimental.pallas import tpu as pltpu
from jax.sharding import PartitionSpec as P

C = 384
W = 64
RD = 2
FD = 2
KEY_BLOCK = 512


epsilon = 1e-06


def scaled_rms(values):
    wide = values.astype(jnp.float32)
    return wide / jnp.sqrt(jnp.mean(wide * wide, axis=-1, keepdims=True) + epsilon)


def attention_kernel(first_ref, cells_ref, wq_ref, wkv_ref, mixed_ref, act_ref):
    width = wq_ref.shape[0]
    scale = 1.0 / math.sqrt(width)
    count = cells_ref.shape[1]
    own = mixed_ref.shape[1]
    line = (act_ref.shape[1] - own) // 2
    frame_rows = count // line
    first = first_ref[0]
    top = jnp.maximum(first, 0) * line
    below = jnp.minimum(first + 1 + own // line, frame_rows - 1) * line
    feats = jnp.concatenate(
        [
            cells_ref[0, pl.ds(top, line), :],
            cells_ref[0, pl.ds((first + 1) * line, own), :],
            cells_ref[0, pl.ds(below, line), :],
        ],
        axis=0,
    ).astype(jnp.float32)
    queries = jnp.dot(
        scaled_rms(feats).astype(jnp.bfloat16), wq_ref[...], preferred_element_type=jnp.float32
    ).astype(jnp.bfloat16)
    block = min(count, KEY_BLOCK)

    def fold(step, carry):
        run_max, run_total, run_acc = carry
        cells = cells_ref[0, pl.ds(step * block, block), :]
        keyvals = jnp.dot(
            scaled_rms(cells).astype(jnp.bfloat16), wkv_ref[...], preferred_element_type=jnp.float32
        ).astype(jnp.bfloat16)
        scores = (
            lax.dot_general(
                queries,
                keyvals[:, :width],
                (((1,), (1,)), ((), ())),
                preferred_element_type=jnp.float32,
            )
            * scale
        )
        new_max = jnp.maximum(run_max, jnp.max(scores, axis=-1, keepdims=True))
        factor = jnp.exp(run_max - new_max)
        powers = jnp.exp(scores - new_max)
        run_total = run_total * factor + jnp.sum(powers, axis=-1, keepdims=True)
        run_acc = run_acc * factor + jnp.dot(
            powers.astype(jnp.bfloat16), keyvals[:, width:], preferred_element_type=jnp.float32
        )
        return new_max, run_total, run_acc

    rows = feats.shape[0]
    carry = (
        jnp.full((rows, 1), -jnp.inf, jnp.float32),
        jnp.zeros((rows, 1), jnp.float32),
        jnp.zeros((rows, width), jnp.float32),
    )
    for step in range(count // block):
        carry = fold(step, carry)
    _, run_total, run_acc = carry
    mixed = (feats + run_acc / run_total).astype(jnp.bfloat16)
    mixed_ref[0] = mixed[line : line + own]
    normed = scaled_rms(mixed)
    row_of = lax.broadcasted_iota(jnp.int32, (rows, width), 0) // line + first
    inside = (row_of >= 0) & (row_of < frame_rows)
    act_ref[0] = jnp.where(inside, normed / (1.0 + jnp.exp(-normed)), 0.0).astype(jnp.bfloat16)


def attend_frames(first, cells, ext_rows, w_query, w_keyval):
    frames, count, width = cells.shape
    own = ext_rows - 2 * (ext_rows // (RD + 2))
    fixed = lambda f, first_ref: (0, 0)
    per_frame = lambda f, first_ref: (f, 0, 0)
    grid_spec = pltpu.PrefetchScalarGridSpec(
        num_scalar_prefetch=1,
        grid=(frames,),
        in_specs=[
            pl.BlockSpec((1, count, width), per_frame),
            pl.BlockSpec(w_query.shape, fixed),
            pl.BlockSpec(w_keyval.shape, fixed),
        ],
        out_specs=[
            pl.BlockSpec((1, own, width), per_frame),
            pl.BlockSpec((1, ext_rows, width), per_frame),
        ],
    )
    return pl.pallas_call(
        attention_kernel,
        grid_spec=grid_spec,
        out_shape=[
            jax.ShapeDtypeStruct((frames, own, width), jnp.bfloat16),
            jax.ShapeDtypeStruct((frames, ext_rows, width), jnp.bfloat16),
        ],
    )(first, cells, w_query, w_keyval)


def timed_conv(frames, kernel, time_pad):
    return lax.conv_general_dilated(
        frames[None],
        kernel,
        (1, 1, 1),
        (time_pad, (0, 0), (1, 1)),
        dimension_numbers=("NDHWC", "DHWIO", "NDHWC"),
        preferred_element_type=jnp.float32,
    )[0]


def local(latent_tiles, route, w_query, w_keyval, conv_weight):
    patch_count = lax.axis_size("patch")
    patch_index = lax.axis_index("patch")
    chan_count = lax.axis_size("chan")
    chan_index = lax.axis_index("chan")
    span_count = lax.axis_size("span")
    table = route[0]
    block = latent_tiles.shape[1]
    share = block // chan_count
    own_share = lax.dynamic_slice_in_dim(latent_tiles, chan_index * share, share, 1)
    every_tile = lax.all_gather(own_share, ("patch", "chan"), axis=1, tiled=True)[0]
    tile_total = every_tile.shape[0]
    rows = patch_count * RD
    per_owner = tile_total // patch_count
    per_frame = per_owner // FD
    owner = table // per_owner
    spot = table % per_owner
    dest = (spot // per_frame) * (tile_total // FD) + owner * per_frame + spot % per_frame
    slots = jnp.arange(tile_total, dtype=jnp.int32)
    one_hot = (slots[:, None] == dest[None, :]).astype(jnp.bfloat16)
    placed = jnp.dot(
        one_hot, every_tile.reshape(tile_total, -1), preferred_element_type=jnp.float32
    ).astype(jnp.bfloat16)
    whole = placed.reshape(FD, rows, W, C)
    first = jnp.reshape(patch_index * RD - 1, (1,)).astype(jnp.int32)
    mixed_own, activated = attend_frames(
        first, whole.reshape(FD, rows * W, C), (RD + 2) * W, w_query, w_keyval
    )
    activated = activated.reshape(FD, RD + 2, W, C)
    to_next = timed_conv(activated, conv_weight[:2], (0, 1)).astype(jnp.bfloat16)
    pairs = [(i, i + 1) for i in range(span_count - 1)]
    from_prev = lax.ppermute(to_next, "span", pairs)
    own_sum = timed_conv(activated, conv_weight[1:], (1, 0))
    out_width = conv_weight.shape[-1]
    own_rows = mixed_own.reshape(FD, RD, W, C)
    own_channels = lax.dynamic_slice_in_dim(own_rows, chan_index * out_width, out_width, 3)
    total = own_channels.astype(jnp.float32) + own_sum + from_prev.astype(jnp.float32)
    return total.astype(jnp.bfloat16)


def solution(mesh):
    placed = (
        P(("clips", "span"), "patch", None, None),
        P(("clips", "span"), None),
        P(),
        P(),
        P(None, None, None, None, "chan"),
    )
    return jax.shard_map(
        local,
        mesh=mesh,
        in_specs=placed,
        out_specs=P(("clips", "span"), "patch", None, "chan"),
        check_vma=False,
    )
```

```python
import math

import jax
import jax.numpy as jnp
from jax import lax
from jax.experimental import pallas as pl
from jax.experimental.pallas import tpu as pltpu
from jax.sharding import PartitionSpec as P

C = 384
W = 64
RD = 2
FD = 2
KEY_BLOCK = 512


epsilon = 1e-06


def scaled_rms(values):
    wide = values.astype(jnp.float32)
    return wide / jnp.sqrt(jnp.mean(wide * wide, axis=-1, keepdims=True) + epsilon)


def attention_kernel(first_ref, tiles_ref, wq_ref, wkv_ref, mixed_ref, act_ref):
    width = wq_ref.shape[0]
    scale = 1.0 / math.sqrt(width)
    cell = tiles_ref.shape[2] // width
    own = mixed_ref.shape[1]
    line = (act_ref.shape[1] - own) // 2
    across = line // cell
    count = tiles_ref.shape[1] * cell
    frame_rows = count // line
    first = first_ref[0]
    top = jnp.maximum(first, 0) * across
    below = jnp.minimum(first + 1 + own // line, frame_rows - 1) * across
    picked = jnp.concatenate(
        [
            tiles_ref[0, pl.ds(top, across), :],
            tiles_ref[0, pl.ds((first + 1) * across, own // cell), :],
            tiles_ref[0, pl.ds(below, across), :],
        ],
        axis=0,
    )
    rows = act_ref.shape[1]
    target = lax.broadcasted_iota(jnp.int32, (rows, rows // cell), 0)
    source = lax.broadcasted_iota(jnp.int32, (rows, rows // cell), 1)
    feats = None
    for i in range(cell):
        spread = ((source == target // cell) & (target % cell == i)).astype(jnp.bfloat16)
        part = jnp.dot(
            spread, picked[:, i * width : (i + 1) * width], preferred_element_type=jnp.float32
        )
        feats = part if feats is None else feats + part
    queries = jnp.dot(
        scaled_rms(feats).astype(jnp.bfloat16), wq_ref[...], preferred_element_type=jnp.float32
    ).astype(jnp.bfloat16)
    block = min(count, KEY_BLOCK)
    chunk = block // cell

    def fold(step, carry):
        run_max, run_total, run_acc = carry
        group = tiles_ref[0, pl.ds(step * chunk, chunk), :]
        cells = jnp.concatenate(
            [group[:, i * width : (i + 1) * width] for i in range(cell)], axis=0
        )
        keyvals = jnp.dot(
            scaled_rms(cells).astype(jnp.bfloat16), wkv_ref[...], preferred_element_type=jnp.float32
        ).astype(jnp.bfloat16)
        scores = (
            lax.dot_general(
                queries,
                keyvals[:, :width],
                (((1,), (1,)), ((), ())),
                preferred_element_type=jnp.float32,
            )
            * scale
        )
        new_max = jnp.maximum(run_max, jnp.max(scores, axis=-1, keepdims=True))
        factor = jnp.exp(run_max - new_max)
        powers = jnp.exp(scores - new_max)
        run_total = run_total * factor + jnp.sum(powers, axis=-1, keepdims=True)
        run_acc = run_acc * factor + jnp.dot(
            powers.astype(jnp.bfloat16), keyvals[:, width:], preferred_element_type=jnp.float32
        )
        return new_max, run_total, run_acc

    carry = (
        jnp.full((rows, 1), -jnp.inf, jnp.float32),
        jnp.zeros((rows, 1), jnp.float32),
        jnp.zeros((rows, width), jnp.float32),
    )
    for step in range(count // block):
        carry = fold(step, carry)
    _, run_total, run_acc = carry
    mixed = (feats + run_acc / run_total).astype(jnp.bfloat16)
    mixed_ref[0] = mixed[line : line + own]
    normed = scaled_rms(mixed)
    row_of = lax.broadcasted_iota(jnp.int32, (rows, width), 0) // line + first
    inside = (row_of >= 0) & (row_of < frame_rows)
    act_ref[0] = jnp.where(inside, normed / (1.0 + jnp.exp(-normed)), 0.0).astype(jnp.bfloat16)


def attend_frames(first, tiles, ext_rows, w_query, w_keyval):
    frames, count, packed = tiles.shape
    width = w_query.shape[0]
    own = ext_rows - 2 * (ext_rows // (RD + 2))
    fixed = lambda f, first_ref: (0, 0)
    per_frame = lambda f, first_ref: (f, 0, 0)
    grid_spec = pltpu.PrefetchScalarGridSpec(
        num_scalar_prefetch=1,
        grid=(frames,),
        in_specs=[
            pl.BlockSpec((1, count, packed), per_frame),
            pl.BlockSpec(w_query.shape, fixed),
            pl.BlockSpec(w_keyval.shape, fixed),
        ],
        out_specs=[
            pl.BlockSpec((1, own, width), per_frame),
            pl.BlockSpec((1, ext_rows, width), per_frame),
        ],
    )
    return pl.pallas_call(
        attention_kernel,
        grid_spec=grid_spec,
        out_shape=[
            jax.ShapeDtypeStruct((frames, own, width), jnp.bfloat16),
            jax.ShapeDtypeStruct((frames, ext_rows, width), jnp.bfloat16),
        ],
    )(first, tiles, w_query, w_keyval)


def timed_conv(frames, kernel, time_pad):
    return lax.conv_general_dilated(
        frames[None],
        kernel,
        (1, 1, 1),
        (time_pad, (0, 0), (1, 1)),
        dimension_numbers=("NDHWC", "DHWIO", "NDHWC"),
        preferred_element_type=jnp.float32,
    )[0]


def local(latent_tiles, route, w_query, w_keyval, conv_weight):
    patch_count = lax.axis_size("patch")
    patch_index = lax.axis_index("patch")
    chan_count = lax.axis_size("chan")
    chan_index = lax.axis_index("chan")
    span_count = lax.axis_size("span")
    table = route[0]
    block = latent_tiles.shape[1]
    share = block // chan_count
    own_share = lax.dynamic_slice_in_dim(latent_tiles, chan_index * share, share, 1)
    every_tile = lax.all_gather(own_share, ("patch", "chan"), axis=1, tiled=True)[0]
    tile_total = every_tile.shape[0]
    rows = patch_count * RD
    per_owner = tile_total // patch_count
    per_frame = per_owner // FD
    owner = table // per_owner
    spot = table % per_owner
    dest = (spot // per_frame) * (tile_total // FD) + owner * per_frame + spot % per_frame
    slots = jnp.arange(tile_total, dtype=jnp.int32)
    one_hot = (slots[:, None] == dest[None, :]).astype(jnp.bfloat16)
    placed = jnp.dot(
        one_hot, every_tile.reshape(tile_total, -1), preferred_element_type=jnp.float32
    ).astype(jnp.bfloat16)
    first = jnp.reshape(patch_index * RD - 1, (1,)).astype(jnp.int32)
    mixed_own, activated = attend_frames(
        first, placed.reshape(FD, tile_total // FD, -1), (RD + 2) * W, w_query, w_keyval
    )
    activated = activated.reshape(FD, RD + 2, W, C)
    to_next = timed_conv(activated, conv_weight[:2], (0, 1)).astype(jnp.bfloat16)
    pairs = [(i, i + 1) for i in range(span_count - 1)]
    from_prev = lax.ppermute(to_next, "span", pairs)
    own_sum = timed_conv(activated, conv_weight[1:], (1, 0))
    out_width = conv_weight.shape[-1]
    own_rows = mixed_own.reshape(FD, RD, W, C)
    own_channels = lax.dynamic_slice_in_dim(own_rows, chan_index * out_width, out_width, 3)
    total = own_channels.astype(jnp.float32) + own_sum + from_prev.astype(jnp.float32)
    return total.astype(jnp.bfloat16)


def solution(mesh):
    placed = (
        P(("clips", "span"), "patch", None, None),
        P(("clips", "span"), None),
        P(),
        P(),
        P(None, None, None, None, "chan"),
    )
    return jax.shard_map(
        local,
        mesh=mesh,
        in_specs=placed,
        out_specs=P(("clips", "span"), "patch", None, "chan"),
        check_vma=False,
    )
```

```python
import math

import jax
import jax.numpy as jnp
from jax import lax
from jax.experimental import pallas as pl
from jax.experimental.pallas import tpu as pltpu
from jax.sharding import PartitionSpec as P

C = 384
W = 64
RD = 2
FD = 2
KEY_BLOCK = 512


epsilon = 1e-06


def scaled_rms(values):
    wide = values.astype(jnp.float32)
    return wide / jnp.sqrt(jnp.mean(wide * wide, axis=-1, keepdims=True) + epsilon)


def attention_kernel(first_ref, cells_ref, wq_ref, wkv_ref, mixed_ref, act_ref):
    width = wq_ref.shape[0]
    scale = 1.0 / math.sqrt(width)
    count = cells_ref.shape[1]
    own = mixed_ref.shape[1]
    line = (act_ref.shape[1] - own) // 2
    frame_rows = count // line
    first = first_ref[0]
    top = jnp.maximum(first, 0) * line
    below = jnp.minimum(first + 1 + own // line, frame_rows - 1) * line
    feats = jnp.concatenate(
        [
            cells_ref[0, pl.ds(top, line), :],
            cells_ref[0, pl.ds((first + 1) * line, own), :],
            cells_ref[0, pl.ds(below, line), :],
        ],
        axis=0,
    ).astype(jnp.float32)
    queries = jnp.dot(
        scaled_rms(feats).astype(jnp.bfloat16), wq_ref[...], preferred_element_type=jnp.float32
    ).astype(jnp.bfloat16)
    block = min(count, KEY_BLOCK)

    def fold(step, carry):
        run_max, run_total, run_acc = carry
        cells = cells_ref[0, pl.ds(step * block, block), :]
        keyvals = jnp.dot(
            scaled_rms(cells).astype(jnp.bfloat16), wkv_ref[...], preferred_element_type=jnp.float32
        ).astype(jnp.bfloat16)
        scores = (
            lax.dot_general(
                queries,
                keyvals[:, :width],
                (((1,), (1,)), ((), ())),
                preferred_element_type=jnp.float32,
            )
            * scale
        )
        new_max = jnp.maximum(run_max, jnp.max(scores, axis=-1, keepdims=True))
        factor = jnp.exp(run_max - new_max)
        powers = jnp.exp(scores - new_max)
        run_total = run_total * factor + jnp.sum(powers, axis=-1, keepdims=True)
        run_acc = run_acc * factor + jnp.dot(
            powers.astype(jnp.bfloat16), keyvals[:, width:], preferred_element_type=jnp.float32
        )
        return new_max, run_total, run_acc

    rows = feats.shape[0]
    carry = (
        jnp.full((rows, 1), -jnp.inf, jnp.float32),
        jnp.zeros((rows, 1), jnp.float32),
        jnp.zeros((rows, width), jnp.float32),
    )
    for step in range(count // block):
        carry = fold(step, carry)
    _, run_total, run_acc = carry
    mixed = (feats + run_acc / run_total).astype(jnp.bfloat16)
    mixed_ref[0] = mixed[line : line + own]
    normed = scaled_rms(mixed)
    row_of = lax.broadcasted_iota(jnp.int32, (rows, width), 0) // line + first
    inside = (row_of >= 0) & (row_of < frame_rows)
    act_ref[0] = jnp.where(inside, normed / (1.0 + jnp.exp(-normed)), 0.0).astype(jnp.bfloat16)


def attend_frames(first, cells, ext_rows, w_query, w_keyval):
    frames, count, width = cells.shape
    own = ext_rows - 2 * (ext_rows // (RD + 2))
    fixed = lambda f, first_ref: (0, 0)
    per_frame = lambda f, first_ref: (f, 0, 0)
    grid_spec = pltpu.PrefetchScalarGridSpec(
        num_scalar_prefetch=1,
        grid=(frames,),
        in_specs=[
            pl.BlockSpec((1, count, width), per_frame),
            pl.BlockSpec(w_query.shape, fixed),
            pl.BlockSpec(w_keyval.shape, fixed),
        ],
        out_specs=[
            pl.BlockSpec((1, own, width), per_frame),
            pl.BlockSpec((1, ext_rows, width), per_frame),
        ],
    )
    return pl.pallas_call(
        attention_kernel,
        grid_spec=grid_spec,
        out_shape=[
            jax.ShapeDtypeStruct((frames, own, width), jnp.bfloat16),
            jax.ShapeDtypeStruct((frames, ext_rows, width), jnp.bfloat16),
        ],
    )(first, cells, w_query, w_keyval)


def timed_conv(frames, kernel, time_pad):
    return lax.conv_general_dilated(
        frames[None],
        kernel,
        (1, 1, 1),
        (time_pad, (0, 0), (1, 1)),
        dimension_numbers=("NDHWC", "DHWIO", "NDHWC"),
        preferred_element_type=jnp.float32,
    )[0]


def local(latent_tiles, route, w_query, w_keyval, conv_weight):
    patch_count = lax.axis_size("patch")
    patch_index = lax.axis_index("patch")
    chan_count = lax.axis_size("chan")
    chan_index = lax.axis_index("chan")
    span_count = lax.axis_size("span")
    table = route[0]
    block = latent_tiles.shape[1]
    share = block // chan_count
    own_share = lax.dynamic_slice_in_dim(latent_tiles, chan_index * share, share, 1)
    every_tile = lax.all_gather(own_share, ("patch", "chan"), axis=1, tiled=True)[0]
    tile_total = every_tile.shape[0]
    rows = patch_count * RD
    per_owner = tile_total // patch_count
    per_frame = per_owner // FD
    owner = table // per_owner
    spot = table % per_owner
    dest = (spot // per_frame) * (tile_total // FD) + owner * per_frame + spot % per_frame
    slots = jnp.arange(tile_total, dtype=jnp.int32)
    one_hot = (slots[:, None] == dest[None, :]).astype(jnp.bfloat16)
    placed = jnp.dot(
        one_hot, every_tile.reshape(tile_total, -1), preferred_element_type=jnp.float32
    ).astype(jnp.bfloat16)
    whole = placed.reshape(FD, rows, W, C)
    first = jnp.reshape(patch_index * RD - 1, (1,)).astype(jnp.int32)
    mixed_own, activated = attend_frames(
        first, whole.reshape(FD, rows * W, C), (RD + 2) * W, w_query, w_keyval
    )
    activated = activated.reshape(FD, RD + 2, W, C)
    to_next = timed_conv(activated, conv_weight[:2], (0, 1)).astype(jnp.bfloat16)
    pairs = [(i, i + 1) for i in range(span_count - 1)]
    from_prev = lax.ppermute(to_next, "span", pairs)
    own_sum = timed_conv(activated, conv_weight[1:], (1, 0))
    out_width = conv_weight.shape[-1]
    own_rows = mixed_own.reshape(FD, RD, W, C)
    own_channels = lax.dynamic_slice_in_dim(own_rows, chan_index * out_width, out_width, 3)
    base = lax.optimization_barrier(own_channels.astype(jnp.float32) + own_sum)
    return (base + from_prev.astype(jnp.float32)).astype(jnp.bfloat16)


def solution(mesh):
    placed = (
        P(("clips", "span"), "patch", None, None),
        P(("clips", "span"), None),
        P(),
        P(),
        P(None, None, None, None, "chan"),
    )
    return jax.shard_map(
        local,
        mesh=mesh,
        in_specs=placed,
        out_specs=P(("clips", "span"), "patch", None, "chan"),
        check_vma=False,
    )
```

```python
import math

import jax
import jax.numpy as jnp
from jax import lax
from jax.experimental import pallas as pl
from jax.experimental.pallas import tpu as pltpu
from jax.sharding import PartitionSpec as P

C = 384
W = 64
RD = 2
FD = 2
KEY_BLOCK = 512


epsilon = 1e-06


def scaled_rms(values):
    wide = values.astype(jnp.float32)
    return wide / jnp.sqrt(jnp.mean(wide * wide, axis=-1, keepdims=True) + epsilon)


def attention_kernel(first_ref, cells_ref, wq_ref, wkv_ref, mixed_ref, act_ref):
    width = wq_ref.shape[0]
    scale = 1.0 / math.sqrt(width)
    count = cells_ref.shape[1]
    own = mixed_ref.shape[1]
    line = (act_ref.shape[1] - own) // 2
    frame_rows = count // line
    first = first_ref[0]
    top = jnp.maximum(first, 0) * line
    below = jnp.minimum(first + 1 + own // line, frame_rows - 1) * line
    feats = jnp.concatenate(
        [
            cells_ref[0, pl.ds(top, line), :],
            cells_ref[0, pl.ds((first + 1) * line, own), :],
            cells_ref[0, pl.ds(below, line), :],
        ],
        axis=0,
    ).astype(jnp.float32)
    queries = jnp.dot(
        scaled_rms(feats).astype(jnp.bfloat16), wq_ref[...], preferred_element_type=jnp.float32
    ).astype(jnp.bfloat16)
    block = min(count, KEY_BLOCK)

    def fold(step, carry):
        run_max, run_total, run_acc = carry
        cells = cells_ref[0, pl.ds(step * block, block), :]
        keyvals = jnp.dot(
            scaled_rms(cells).astype(jnp.bfloat16), wkv_ref[...], preferred_element_type=jnp.float32
        ).astype(jnp.bfloat16)
        scores = (
            lax.dot_general(
                queries,
                keyvals[:, :width],
                (((1,), (1,)), ((), ())),
                preferred_element_type=jnp.float32,
            )
            * scale
        )
        new_max = jnp.maximum(run_max, jnp.max(scores, axis=-1, keepdims=True))
        factor = jnp.exp(run_max - new_max)
        powers = jnp.exp(scores - new_max)
        run_total = run_total * factor + jnp.sum(powers, axis=-1, keepdims=True)
        run_acc = run_acc * factor + jnp.dot(
            powers.astype(jnp.bfloat16), keyvals[:, width:], preferred_element_type=jnp.float32
        )
        return new_max, run_total, run_acc

    rows = feats.shape[0]
    carry = (
        jnp.full((rows, 1), -jnp.inf, jnp.float32),
        jnp.zeros((rows, 1), jnp.float32),
        jnp.zeros((rows, width), jnp.float32),
    )
    for step in range(count // block):
        carry = fold(step, carry)
    _, run_total, run_acc = carry
    mixed = (feats + run_acc / run_total).astype(jnp.bfloat16)
    mixed_ref[0] = mixed[line : line + own]
    normed = scaled_rms(mixed)
    row_of = lax.broadcasted_iota(jnp.int32, (rows, width), 0) // line + first
    inside = (row_of >= 0) & (row_of < frame_rows)
    act_ref[0] = jnp.where(inside, normed / (1.0 + jnp.exp(-normed)), 0.0).astype(jnp.bfloat16)


def attend_frames(first, cells, ext_rows, w_query, w_keyval):
    frames, count, width = cells.shape
    own = ext_rows - 2 * (ext_rows // (RD + 2))
    fixed = lambda f, first_ref: (0, 0)
    per_frame = lambda f, first_ref: (f, 0, 0)
    grid_spec = pltpu.PrefetchScalarGridSpec(
        num_scalar_prefetch=1,
        grid=(frames,),
        in_specs=[
            pl.BlockSpec((1, count, width), per_frame),
            pl.BlockSpec(w_query.shape, fixed),
            pl.BlockSpec(w_keyval.shape, fixed),
        ],
        out_specs=[
            pl.BlockSpec((1, own, width), per_frame),
            pl.BlockSpec((1, ext_rows, width), per_frame),
        ],
    )
    block_bytes = count * width * 2
    return pl.pallas_call(
        attention_kernel,
        grid_spec=grid_spec,
        compiler_params=pltpu.CompilerParams(vmem_limit_bytes=6 * block_bytes + (6 << 20)),
        out_shape=[
            jax.ShapeDtypeStruct((frames, own, width), jnp.bfloat16),
            jax.ShapeDtypeStruct((frames, ext_rows, width), jnp.bfloat16),
        ],
    )(first, cells, w_query, w_keyval)


def timed_conv(frames, kernel, time_pad):
    return lax.conv_general_dilated(
        frames[None],
        kernel,
        (1, 1, 1),
        (time_pad, (0, 0), (1, 1)),
        dimension_numbers=("NDHWC", "DHWIO", "NDHWC"),
        preferred_element_type=jnp.float32,
    )[0]


def local(latent_tiles, route, w_query, w_keyval, conv_weight):
    patch_count = lax.axis_size("patch")
    patch_index = lax.axis_index("patch")
    chan_count = lax.axis_size("chan")
    chan_index = lax.axis_index("chan")
    span_count = lax.axis_size("span")
    table = route[0]
    block = latent_tiles.shape[1]
    share = block // chan_count
    own_share = lax.dynamic_slice_in_dim(latent_tiles, chan_index * share, share, 1)
    every_tile = lax.all_gather(own_share, ("patch", "chan"), axis=1, tiled=True)[0]
    tile_total = every_tile.shape[0]
    rows = patch_count * RD
    per_owner = tile_total // patch_count
    per_frame = per_owner // FD
    owner = table // per_owner
    spot = table % per_owner
    dest = (spot // per_frame) * (tile_total // FD) + owner * per_frame + spot % per_frame
    slots = jnp.arange(tile_total, dtype=jnp.int32)
    one_hot = (slots[:, None] == dest[None, :]).astype(jnp.bfloat16)
    placed = jnp.dot(
        one_hot, every_tile.reshape(tile_total, -1), preferred_element_type=jnp.float32
    ).astype(jnp.bfloat16)
    whole = placed.reshape(FD, rows, W, C)
    first = jnp.reshape(patch_index * RD - 1, (1,)).astype(jnp.int32)
    mixed_own, activated = attend_frames(
        first, whole.reshape(FD, rows * W, C), (RD + 2) * W, w_query, w_keyval
    )
    activated = activated.reshape(FD, RD + 2, W, C)
    to_next = timed_conv(activated, conv_weight[:2], (0, 1)).astype(jnp.bfloat16)
    pairs = [(i, i + 1) for i in range(span_count - 1)]
    from_prev = lax.ppermute(to_next, "span", pairs)
    own_sum = timed_conv(activated, conv_weight[1:], (1, 0))
    out_width = conv_weight.shape[-1]
    own_rows = mixed_own.reshape(FD, RD, W, C)
    own_channels = lax.dynamic_slice_in_dim(own_rows, chan_index * out_width, out_width, 3)
    base = lax.optimization_barrier(own_channels.astype(jnp.float32) + own_sum)
    return (base + from_prev.astype(jnp.float32)).astype(jnp.bfloat16)


def solution(mesh):
    placed = (
        P(("clips", "span"), "patch", None, None),
        P(("clips", "span"), None),
        P(),
        P(),
        P(None, None, None, None, "chan"),
    )
    return jax.shard_map(
        local,
        mesh=mesh,
        in_specs=placed,
        out_specs=P(("clips", "span"), "patch", None, "chan"),
        check_vma=False,
    )
```

```python
import math

import jax
import jax.numpy as jnp
from jax import lax
from jax.experimental import pallas as pl
from jax.experimental.pallas import tpu as pltpu
from jax.sharding import PartitionSpec as P

C = 384
W = 64
RD = 2
FD = 2
KEY_BLOCK = 512


epsilon = 1e-06


def scaled_rms(values):
    wide = values.astype(jnp.float32)
    return wide / jnp.sqrt(jnp.mean(wide * wide, axis=-1, keepdims=True) + epsilon)


def attention_kernel(first_ref, cells_ref, wq_ref, wkv_ref, mixed_ref, act_ref):
    width = wq_ref.shape[0]
    scale = 1.0 / math.sqrt(width)
    count = cells_ref.shape[1]
    own = mixed_ref.shape[1]
    line = (act_ref.shape[1] - own) // 2
    frame_rows = count // line
    first = first_ref[0]
    top = jnp.maximum(first, 0) * line
    below = jnp.minimum(first + 1 + own // line, frame_rows - 1) * line
    feats = jnp.concatenate(
        [
            cells_ref[0, pl.ds(top, line), :],
            cells_ref[0, pl.ds((first + 1) * line, own), :],
            cells_ref[0, pl.ds(below, line), :],
        ],
        axis=0,
    ).astype(jnp.float32)
    queries = jnp.dot(
        scaled_rms(feats).astype(jnp.bfloat16), wq_ref[...], preferred_element_type=jnp.float32
    ).astype(jnp.bfloat16)
    block = min(count, KEY_BLOCK)

    def fold(step, carry):
        run_max, run_total, run_acc = carry
        cells = cells_ref[0, pl.ds(step * block, block), :]
        keyvals = jnp.dot(
            scaled_rms(cells).astype(jnp.bfloat16), wkv_ref[...], preferred_element_type=jnp.float32
        ).astype(jnp.bfloat16)
        scores = (
            lax.dot_general(
                queries,
                keyvals[:, :width],
                (((1,), (1,)), ((), ())),
                preferred_element_type=jnp.float32,
            )
            * scale
        )
        new_max = jnp.maximum(run_max, jnp.max(scores, axis=-1, keepdims=True))
        factor = jnp.exp(run_max - new_max)
        powers = jnp.exp(scores - new_max)
        run_total = run_total * factor + jnp.sum(powers, axis=-1, keepdims=True)
        run_acc = run_acc * factor + jnp.dot(
            powers.astype(jnp.bfloat16), keyvals[:, width:], preferred_element_type=jnp.float32
        )
        return new_max, run_total, run_acc

    rows = feats.shape[0]
    carry = (
        jnp.full((rows, 1), -jnp.inf, jnp.float32),
        jnp.zeros((rows, 1), jnp.float32),
        jnp.zeros((rows, width), jnp.float32),
    )
    for step in range(count // block):
        carry = fold(step, carry)
    _, run_total, run_acc = carry
    mixed = (feats + run_acc / run_total).astype(jnp.bfloat16)
    mixed_ref[0] = mixed[line : line + own]
    normed = scaled_rms(mixed)
    row_of = lax.broadcasted_iota(jnp.int32, (rows, width), 0) // line + first
    inside = (row_of >= 0) & (row_of < frame_rows)
    act_ref[0] = jnp.where(inside, normed / (1.0 + jnp.exp(-normed)), 0.0).astype(jnp.bfloat16)


def attend_frames(first, cells, ext_rows, w_query, w_keyval):
    frames, count, width = cells.shape
    own = ext_rows - 2 * (ext_rows // (RD + 2))
    fixed = lambda f, first_ref: (0, 0)
    per_frame = lambda f, first_ref: (f, 0, 0)
    grid_spec = pltpu.PrefetchScalarGridSpec(
        num_scalar_prefetch=1,
        grid=(frames,),
        in_specs=[
            pl.BlockSpec((1, count, width), per_frame),
            pl.BlockSpec(w_query.shape, fixed),
            pl.BlockSpec(w_keyval.shape, fixed),
        ],
        out_specs=[
            pl.BlockSpec((1, own, width), per_frame),
            pl.BlockSpec((1, ext_rows, width), per_frame),
        ],
    )
    block_bytes = count * width * 2
    return pl.pallas_call(
        attention_kernel,
        grid_spec=grid_spec,
        compiler_params=pltpu.CompilerParams(vmem_limit_bytes=6 * block_bytes + (6 << 20)),
        out_shape=[
            jax.ShapeDtypeStruct((frames, own, width), jnp.bfloat16),
            jax.ShapeDtypeStruct((frames, ext_rows, width), jnp.bfloat16),
        ],
    )(first, cells, w_query, w_keyval)


def timed_conv(frames, kernel, time_pad):
    return lax.conv_general_dilated(
        frames[None],
        kernel,
        (1, 1, 1),
        (time_pad, (0, 0), (1, 1)),
        dimension_numbers=("NDHWC", "DHWIO", "NDHWC"),
        preferred_element_type=jnp.float32,
    )[0]


def gather_tiles(share, patch_count, patch_index):
    if patch_count <= 4:
        got = [share]
        for d in range(1, patch_count):
            shift = [(i, (i + d) % patch_count) for i in range(patch_count)]
            got.append(lax.ppermute(share, "patch", shift))
        order = (patch_index - jnp.arange(patch_count)) % patch_count
        by_patch = jnp.take(jnp.stack(got), order, axis=0)
    else:
        by_patch = lax.all_gather(share, "patch", axis=0, tiled=False)
    both = lax.all_gather(by_patch, "chan", axis=1, tiled=False)
    return both.reshape((-1,) + share.shape[1:])


def local(latent_tiles, route, w_query, w_keyval, conv_weight):
    patch_count = lax.axis_size("patch")
    patch_index = lax.axis_index("patch")
    chan_count = lax.axis_size("chan")
    chan_index = lax.axis_index("chan")
    span_count = lax.axis_size("span")
    table = route[0]
    block = latent_tiles.shape[1]
    share = block // chan_count
    own_share = lax.dynamic_slice_in_dim(latent_tiles, chan_index * share, share, 1)
    every_tile = gather_tiles(own_share[0], patch_count, patch_index)
    tile_total = every_tile.shape[0]
    rows = patch_count * RD
    per_owner = tile_total // patch_count
    per_frame = per_owner // FD
    owner = table // per_owner
    spot = table % per_owner
    dest = (spot // per_frame) * (tile_total // FD) + owner * per_frame + spot % per_frame
    slots = jnp.arange(tile_total, dtype=jnp.int32)
    one_hot = (slots[:, None] == dest[None, :]).astype(jnp.bfloat16)
    placed = jnp.dot(
        one_hot, every_tile.reshape(tile_total, -1), preferred_element_type=jnp.float32
    ).astype(jnp.bfloat16)
    whole = placed.reshape(FD, rows, W, C)
    first = jnp.reshape(patch_index * RD - 1, (1,)).astype(jnp.int32)
    mixed_own, activated = attend_frames(
        first, whole.reshape(FD, rows * W, C), (RD + 2) * W, w_query, w_keyval
    )
    activated = activated.reshape(FD, RD + 2, W, C)
    to_next = timed_conv(activated, conv_weight[:2], (0, 1)).astype(jnp.bfloat16)
    pairs = [(i, i + 1) for i in range(span_count - 1)]
    from_prev = lax.ppermute(to_next, "span", pairs)
    own_sum = timed_conv(activated, conv_weight[1:], (1, 0))
    out_width = conv_weight.shape[-1]
    own_rows = mixed_own.reshape(FD, RD, W, C)
    own_channels = lax.dynamic_slice_in_dim(own_rows, chan_index * out_width, out_width, 3)
    base = lax.optimization_barrier(own_channels.astype(jnp.float32) + own_sum)
    return (base + from_prev.astype(jnp.float32)).astype(jnp.bfloat16)


def solution(mesh):
    placed = (
        P(("clips", "span"), "patch", None, None),
        P(("clips", "span"), None),
        P(),
        P(),
        P(None, None, None, None, "chan"),
    )
    return jax.shard_map(
        local,
        mesh=mesh,
        in_specs=placed,
        out_specs=P(("clips", "span"), "patch", None, "chan"),
        check_vma=False,
    )
```

```python
import math

import jax
import jax.numpy as jnp
from jax import lax
from jax.experimental import pallas as pl
from jax.experimental.pallas import tpu as pltpu
from jax.sharding import PartitionSpec as P

C = 384
W = 64
RD = 2
FD = 2
KEY_BLOCK = 512


epsilon = 1e-06


def scaled_rms(values):
    wide = values.astype(jnp.float32)
    return wide / jnp.sqrt(jnp.mean(wide * wide, axis=-1, keepdims=True) + epsilon)


def attention_kernel(first_ref, cells_ref, wq_ref, wkv_ref, mixed_ref, act_ref):
    width = wq_ref.shape[0]
    scale = 1.0 / math.sqrt(width)
    count = cells_ref.shape[1]
    own = mixed_ref.shape[1]
    line = (act_ref.shape[1] - own) // 2
    frame_rows = count // line
    first = first_ref[0]
    top = jnp.maximum(first, 0) * line
    below = jnp.minimum(first + 1 + own // line, frame_rows - 1) * line
    feats = jnp.concatenate(
        [
            cells_ref[0, pl.ds(top, line), :],
            cells_ref[0, pl.ds((first + 1) * line, own), :],
            cells_ref[0, pl.ds(below, line), :],
        ],
        axis=0,
    ).astype(jnp.float32)
    queries = jnp.dot(
        scaled_rms(feats).astype(jnp.bfloat16), wq_ref[...], preferred_element_type=jnp.float32
    ).astype(jnp.bfloat16)
    block = min(count, KEY_BLOCK)

    def fold(step, carry):
        run_max, run_total, run_acc = carry
        cells = cells_ref[0, pl.ds(step * block, block), :]
        keyvals = jnp.dot(
            scaled_rms(cells).astype(jnp.bfloat16), wkv_ref[...], preferred_element_type=jnp.float32
        ).astype(jnp.bfloat16)
        scores = (
            lax.dot_general(
                queries,
                keyvals[:, :width],
                (((1,), (1,)), ((), ())),
                preferred_element_type=jnp.float32,
            )
            * scale
        )
        new_max = jnp.maximum(run_max, jnp.max(scores, axis=-1, keepdims=True))
        factor = jnp.exp(run_max - new_max)
        powers = jnp.exp(scores - new_max)
        run_total = run_total * factor + jnp.sum(powers, axis=-1, keepdims=True)
        run_acc = run_acc * factor + jnp.dot(
            powers.astype(jnp.bfloat16), keyvals[:, width:], preferred_element_type=jnp.float32
        )
        return new_max, run_total, run_acc

    rows = feats.shape[0]
    carry = (
        jnp.full((rows, 1), -jnp.inf, jnp.float32),
        jnp.zeros((rows, 1), jnp.float32),
        jnp.zeros((rows, width), jnp.float32),
    )
    for step in range(count // block):
        carry = fold(step, carry)
    _, run_total, run_acc = carry
    mixed = (feats + run_acc / run_total).astype(jnp.bfloat16)
    mixed_ref[0] = mixed[line : line + own]
    normed = scaled_rms(mixed)
    row_of = lax.broadcasted_iota(jnp.int32, (rows, width), 0) // line + first
    inside = (row_of >= 0) & (row_of < frame_rows)
    act_ref[0] = jnp.where(inside, normed / (1.0 + jnp.exp(-normed)), 0.0).astype(jnp.bfloat16)


def attend_frames(first, cells, ext_rows, w_query, w_keyval):
    frames, count, width = cells.shape
    own = ext_rows - 2 * (ext_rows // (RD + 2))
    fixed = lambda f, first_ref: (0, 0)
    per_frame = lambda f, first_ref: (f, 0, 0)
    grid_spec = pltpu.PrefetchScalarGridSpec(
        num_scalar_prefetch=1,
        grid=(frames,),
        in_specs=[
            pl.BlockSpec((1, count, width), per_frame),
            pl.BlockSpec(w_query.shape, fixed),
            pl.BlockSpec(w_keyval.shape, fixed),
        ],
        out_specs=[
            pl.BlockSpec((1, own, width), per_frame),
            pl.BlockSpec((1, ext_rows, width), per_frame),
        ],
    )
    block_bytes = count * width * 2
    return pl.pallas_call(
        attention_kernel,
        grid_spec=grid_spec,
        compiler_params=pltpu.CompilerParams(vmem_limit_bytes=6 * block_bytes + (6 << 20)),
        out_shape=[
            jax.ShapeDtypeStruct((frames, own, width), jnp.bfloat16),
            jax.ShapeDtypeStruct((frames, ext_rows, width), jnp.bfloat16),
        ],
    )(first, cells, w_query, w_keyval)


def timed_conv(frames, kernel, time_pad):
    return lax.conv_general_dilated(
        frames[None],
        kernel,
        (1, 1, 1),
        (time_pad, (0, 0), (1, 1)),
        dimension_numbers=("NDHWC", "DHWIO", "NDHWC"),
        preferred_element_type=jnp.float32,
    )[0]


def local(latent_tiles, route, w_query, w_keyval, conv_weight):
    patch_count = lax.axis_size("patch")
    patch_index = lax.axis_index("patch")
    chan_count = lax.axis_size("chan")
    chan_index = lax.axis_index("chan")
    span_count = lax.axis_size("span")
    table = route[0]
    block = latent_tiles.shape[1]
    share = block // chan_count
    own_share = lax.dynamic_slice_in_dim(latent_tiles, chan_index * share, share, 1)
    every_tile = lax.all_gather(own_share, ("patch", "chan"), axis=1, tiled=True)[0]
    every_tile, table = lax.optimization_barrier((every_tile, table))
    tile_total = every_tile.shape[0]
    rows = patch_count * RD
    per_owner = tile_total // patch_count
    per_frame = per_owner // FD
    owner = table // per_owner
    spot = table % per_owner
    dest = (spot // per_frame) * (tile_total // FD) + owner * per_frame + spot % per_frame
    slots = jnp.arange(tile_total, dtype=jnp.int32)
    one_hot = (slots[:, None] == dest[None, :]).astype(jnp.bfloat16)
    placed = jnp.dot(
        one_hot, every_tile.reshape(tile_total, -1), preferred_element_type=jnp.float32
    ).astype(jnp.bfloat16)
    whole = placed.reshape(FD, rows, W, C)
    first = jnp.reshape(patch_index * RD - 1, (1,)).astype(jnp.int32)
    mixed_own, activated = attend_frames(
        first, whole.reshape(FD, rows * W, C), (RD + 2) * W, w_query, w_keyval
    )
    activated = activated.reshape(FD, RD + 2, W, C)
    to_next = timed_conv(activated, conv_weight[:2], (0, 1)).astype(jnp.bfloat16)
    pairs = [(i, i + 1) for i in range(span_count - 1)]
    from_prev = lax.ppermute(to_next, "span", pairs)
    own_sum = timed_conv(activated, conv_weight[1:], (1, 0))
    out_width = conv_weight.shape[-1]
    own_rows = mixed_own.reshape(FD, RD, W, C)
    own_channels = lax.dynamic_slice_in_dim(own_rows, chan_index * out_width, out_width, 3)
    base = lax.optimization_barrier(own_channels.astype(jnp.float32) + own_sum)
    return (base + from_prev.astype(jnp.float32)).astype(jnp.bfloat16)


def solution(mesh):
    placed = (
        P(("clips", "span"), "patch", None, None),
        P(("clips", "span"), None),
        P(),
        P(),
        P(None, None, None, None, "chan"),
    )
    return jax.shard_map(
        local,
        mesh=mesh,
        in_specs=placed,
        out_specs=P(("clips", "span"), "patch", None, "chan"),
        check_vma=False,
    )
```

```python
import math

import jax
import jax.numpy as jnp
from jax import lax
from jax.experimental import pallas as pl
from jax.experimental.pallas import tpu as pltpu
from jax.sharding import PartitionSpec as P

C = 384
W = 64
RD = 2
FD = 2
KEY_BLOCK = 512


epsilon = 1e-06


def scaled_rms(values):
    wide = values.astype(jnp.float32)
    return wide / jnp.sqrt(jnp.mean(wide * wide, axis=-1, keepdims=True) + epsilon)


def attention_kernel(first_ref, cells_ref, wq_ref, wkv_ref, mixed_ref, act_ref):
    for frame in range(cells_ref.shape[0]):
        attend_frame(first_ref, cells_ref, wq_ref, wkv_ref, mixed_ref, act_ref, frame)


def attend_frame(first_ref, cells_ref, wq_ref, wkv_ref, mixed_ref, act_ref, frame):
    width = wq_ref.shape[0]
    scale = 1.0 / math.sqrt(width)
    count = cells_ref.shape[1]
    own = mixed_ref.shape[1]
    line = (act_ref.shape[1] - own) // 2
    frame_rows = count // line
    first = first_ref[0]
    top = jnp.maximum(first, 0) * line
    below = jnp.minimum(first + 1 + own // line, frame_rows - 1) * line
    feats = jnp.concatenate(
        [
            cells_ref[frame, pl.ds(top, line), :],
            cells_ref[frame, pl.ds((first + 1) * line, own), :],
            cells_ref[frame, pl.ds(below, line), :],
        ],
        axis=0,
    ).astype(jnp.float32)
    queries = jnp.dot(
        scaled_rms(feats).astype(jnp.bfloat16), wq_ref[...], preferred_element_type=jnp.float32
    ).astype(jnp.bfloat16)
    block = min(count, KEY_BLOCK)

    def fold(step, carry):
        run_max, run_total, run_acc = carry
        cells = cells_ref[frame, pl.ds(step * block, block), :]
        keyvals = jnp.dot(
            scaled_rms(cells).astype(jnp.bfloat16), wkv_ref[...], preferred_element_type=jnp.float32
        ).astype(jnp.bfloat16)
        scores = (
            lax.dot_general(
                queries,
                keyvals[:, :width],
                (((1,), (1,)), ((), ())),
                preferred_element_type=jnp.float32,
            )
            * scale
        )
        new_max = jnp.maximum(run_max, jnp.max(scores, axis=-1, keepdims=True))
        factor = jnp.exp(run_max - new_max)
        powers = jnp.exp(scores - new_max)
        run_total = run_total * factor + jnp.sum(powers, axis=-1, keepdims=True)
        run_acc = run_acc * factor + jnp.dot(
            powers.astype(jnp.bfloat16), keyvals[:, width:], preferred_element_type=jnp.float32
        )
        return new_max, run_total, run_acc

    rows = feats.shape[0]
    carry = (
        jnp.full((rows, 1), -jnp.inf, jnp.float32),
        jnp.zeros((rows, 1), jnp.float32),
        jnp.zeros((rows, width), jnp.float32),
    )
    for step in range(count // block):
        carry = fold(step, carry)
    _, run_total, run_acc = carry
    mixed = (feats + run_acc / run_total).astype(jnp.bfloat16)
    mixed_ref[frame] = mixed[line : line + own]
    normed = scaled_rms(mixed)
    row_of = lax.broadcasted_iota(jnp.int32, (rows, width), 0) // line + first
    inside = (row_of >= 0) & (row_of < frame_rows)
    act_ref[frame] = jnp.where(inside, normed / (1.0 + jnp.exp(-normed)), 0.0).astype(jnp.bfloat16)


def attend_frames(first, cells, ext_rows, w_query, w_keyval):
    frames, count, width = cells.shape
    own = ext_rows - 2 * (ext_rows // (RD + 2))
    fixed = lambda f, first_ref: (0, 0)
    per_frame = lambda f, first_ref: (f, 0, 0)
    grid_spec = pltpu.PrefetchScalarGridSpec(
        num_scalar_prefetch=1,
        grid=(1,),
        in_specs=[
            pl.BlockSpec((frames, count, width), per_frame),
            pl.BlockSpec(w_query.shape, fixed),
            pl.BlockSpec(w_keyval.shape, fixed),
        ],
        out_specs=[
            pl.BlockSpec((frames, own, width), per_frame),
            pl.BlockSpec((frames, ext_rows, width), per_frame),
        ],
    )
    block_bytes = count * width * 2
    return pl.pallas_call(
        attention_kernel,
        grid_spec=grid_spec,
        compiler_params=pltpu.CompilerParams(vmem_limit_bytes=6 * frames * block_bytes + (6 << 20)),
        out_shape=[
            jax.ShapeDtypeStruct((frames, own, width), jnp.bfloat16),
            jax.ShapeDtypeStruct((frames, ext_rows, width), jnp.bfloat16),
        ],
    )(first, cells, w_query, w_keyval)


def timed_conv(frames, kernel, time_pad):
    return lax.conv_general_dilated(
        frames[None],
        kernel,
        (1, 1, 1),
        (time_pad, (0, 0), (1, 1)),
        dimension_numbers=("NDHWC", "DHWIO", "NDHWC"),
        preferred_element_type=jnp.float32,
    )[0]


def local(latent_tiles, route, w_query, w_keyval, conv_weight):
    patch_count = lax.axis_size("patch")
    patch_index = lax.axis_index("patch")
    chan_count = lax.axis_size("chan")
    chan_index = lax.axis_index("chan")
    span_count = lax.axis_size("span")
    table = route[0]
    block = latent_tiles.shape[1]
    share = block // chan_count
    own_share = lax.dynamic_slice_in_dim(latent_tiles, chan_index * share, share, 1)
    every_tile = lax.all_gather(own_share, ("patch", "chan"), axis=1, tiled=True)[0]
    tile_total = every_tile.shape[0]
    rows = patch_count * RD
    per_owner = tile_total // patch_count
    per_frame = per_owner // FD
    owner = table // per_owner
    spot = table % per_owner
    dest = (spot // per_frame) * (tile_total // FD) + owner * per_frame + spot % per_frame
    slots = jnp.arange(tile_total, dtype=jnp.int32)
    one_hot = (slots[:, None] == dest[None, :]).astype(jnp.bfloat16)
    placed = jnp.dot(
        one_hot, every_tile.reshape(tile_total, -1), preferred_element_type=jnp.float32
    ).astype(jnp.bfloat16)
    whole = placed.reshape(FD, rows, W, C)
    first = jnp.reshape(patch_index * RD - 1, (1,)).astype(jnp.int32)
    mixed_own, activated = attend_frames(
        first, whole.reshape(FD, rows * W, C), (RD + 2) * W, w_query, w_keyval
    )
    activated = activated.reshape(FD, RD + 2, W, C)
    to_next = timed_conv(activated, conv_weight[:2], (0, 1)).astype(jnp.bfloat16)
    pairs = [(i, i + 1) for i in range(span_count - 1)]
    from_prev = lax.ppermute(to_next, "span", pairs)
    own_sum = timed_conv(activated, conv_weight[1:], (1, 0))
    out_width = conv_weight.shape[-1]
    own_rows = mixed_own.reshape(FD, RD, W, C)
    own_channels = lax.dynamic_slice_in_dim(own_rows, chan_index * out_width, out_width, 3)
    base = lax.optimization_barrier(own_channels.astype(jnp.float32) + own_sum)
    return (base + from_prev.astype(jnp.float32)).astype(jnp.bfloat16)


def solution(mesh):
    placed = (
        P(("clips", "span"), "patch", None, None),
        P(("clips", "span"), None),
        P(),
        P(),
        P(None, None, None, None, "chan"),
    )
    return jax.shard_map(
        local,
        mesh=mesh,
        in_specs=placed,
        out_specs=P(("clips", "span"), "patch", None, "chan"),
        check_vma=False,
    )
```

```python
import math

import jax
import jax.numpy as jnp
from jax import lax
from jax.experimental import pallas as pl
from jax.experimental.pallas import tpu as pltpu
from jax.sharding import PartitionSpec as P

C = 384
W = 64
RD = 2
FD = 2
KEY_BLOCK = 512


epsilon = 1e-06


def scaled_rms(values):
    wide = values.astype(jnp.float32)
    return wide / jnp.sqrt(jnp.mean(wide * wide, axis=-1, keepdims=True) + epsilon)


def attention_kernel(first_ref, tiles_ref, wq_ref, wkv_ref, mixed_ref, act_ref):
    for frame in range(tiles_ref.shape[0]):
        attend_frame(first_ref, tiles_ref, wq_ref, wkv_ref, mixed_ref, act_ref, frame)


def attend_frame(first_ref, tiles_ref, wq_ref, wkv_ref, mixed_ref, act_ref, frame):
    width = wq_ref.shape[0]
    scale = 1.0 / math.sqrt(width)
    cell = tiles_ref.shape[2] // width
    own = mixed_ref.shape[1]
    line = (act_ref.shape[1] - own) // 2
    across = line // cell
    count = tiles_ref.shape[1] * cell
    frame_rows = count // line
    first = first_ref[0]
    top = jnp.maximum(first, 0) * across
    below = jnp.minimum(first + 1 + own // line, frame_rows - 1) * across
    picked = jnp.concatenate(
        [
            tiles_ref[frame, pl.ds(top, across), :],
            tiles_ref[frame, pl.ds((first + 1) * across, own // cell), :],
            tiles_ref[frame, pl.ds(below, across), :],
        ],
        axis=0,
    )
    rows = act_ref.shape[1]
    target = lax.broadcasted_iota(jnp.int32, (rows, rows // cell), 0)
    source = lax.broadcasted_iota(jnp.int32, (rows, rows // cell), 1)
    feats = None
    for i in range(cell):
        spread = ((source == target // cell) & (target % cell == i)).astype(jnp.bfloat16)
        part = jnp.dot(
            spread, picked[:, i * width : (i + 1) * width], preferred_element_type=jnp.float32
        )
        feats = part if feats is None else feats + part
    queries = jnp.dot(
        scaled_rms(feats).astype(jnp.bfloat16), wq_ref[...], preferred_element_type=jnp.float32
    ).astype(jnp.bfloat16)
    block = min(count, KEY_BLOCK)
    chunk = block // cell

    def fold(step, carry):
        run_max, run_total, run_acc = carry
        group = tiles_ref[frame, pl.ds(step * chunk, chunk), :]
        cells = jnp.concatenate(
            [group[:, i * width : (i + 1) * width] for i in range(cell)], axis=0
        )
        keyvals = jnp.dot(
            scaled_rms(cells).astype(jnp.bfloat16), wkv_ref[...], preferred_element_type=jnp.float32
        ).astype(jnp.bfloat16)
        scores = (
            lax.dot_general(
                queries,
                keyvals[:, :width],
                (((1,), (1,)), ((), ())),
                preferred_element_type=jnp.float32,
            )
            * scale
        )
        new_max = jnp.maximum(run_max, jnp.max(scores, axis=-1, keepdims=True))
        factor = jnp.exp(run_max - new_max)
        powers = jnp.exp(scores - new_max)
        run_total = run_total * factor + jnp.sum(powers, axis=-1, keepdims=True)
        run_acc = run_acc * factor + jnp.dot(
            powers.astype(jnp.bfloat16), keyvals[:, width:], preferred_element_type=jnp.float32
        )
        return new_max, run_total, run_acc

    carry = (
        jnp.full((rows, 1), -jnp.inf, jnp.float32),
        jnp.zeros((rows, 1), jnp.float32),
        jnp.zeros((rows, width), jnp.float32),
    )
    for step in range(count // block):
        carry = fold(step, carry)
    _, run_total, run_acc = carry
    mixed = (feats + run_acc / run_total).astype(jnp.bfloat16)
    mixed_ref[frame] = mixed[line : line + own]
    normed = scaled_rms(mixed)
    row_of = lax.broadcasted_iota(jnp.int32, (rows, width), 0) // line + first
    inside = (row_of >= 0) & (row_of < frame_rows)
    act_ref[frame] = jnp.where(inside, normed / (1.0 + jnp.exp(-normed)), 0.0).astype(jnp.bfloat16)


def attend_frames(first, tiles, ext_rows, w_query, w_keyval):
    frames, count, packed = tiles.shape
    width = w_query.shape[0]
    own = ext_rows - 2 * (ext_rows // (RD + 2))
    fixed = lambda f, first_ref: (0, 0)
    per_frame = lambda f, first_ref: (f, 0, 0)
    grid_spec = pltpu.PrefetchScalarGridSpec(
        num_scalar_prefetch=1,
        grid=(1,),
        in_specs=[
            pl.BlockSpec((frames, count, packed), per_frame),
            pl.BlockSpec(w_query.shape, fixed),
            pl.BlockSpec(w_keyval.shape, fixed),
        ],
        out_specs=[
            pl.BlockSpec((frames, own, width), per_frame),
            pl.BlockSpec((frames, ext_rows, width), per_frame),
        ],
    )
    block_bytes = count * packed * 2
    return pl.pallas_call(
        attention_kernel,
        grid_spec=grid_spec,
        compiler_params=pltpu.CompilerParams(vmem_limit_bytes=6 * frames * block_bytes + (6 << 20)),
        out_shape=[
            jax.ShapeDtypeStruct((frames, own, width), jnp.bfloat16),
            jax.ShapeDtypeStruct((frames, ext_rows, width), jnp.bfloat16),
        ],
    )(first, tiles, w_query, w_keyval)


def timed_conv(frames, kernel, time_pad):
    return lax.conv_general_dilated(
        frames[None],
        kernel,
        (1, 1, 1),
        (time_pad, (0, 0), (1, 1)),
        dimension_numbers=("NDHWC", "DHWIO", "NDHWC"),
        preferred_element_type=jnp.float32,
    )[0]


def local(latent_tiles, route, w_query, w_keyval, conv_weight):
    patch_count = lax.axis_size("patch")
    patch_index = lax.axis_index("patch")
    chan_count = lax.axis_size("chan")
    chan_index = lax.axis_index("chan")
    span_count = lax.axis_size("span")
    table = route[0]
    block = latent_tiles.shape[1]
    share = block // chan_count
    own_share = lax.dynamic_slice_in_dim(latent_tiles, chan_index * share, share, 1)
    every_tile = lax.all_gather(own_share, ("patch", "chan"), axis=1, tiled=True)[0]
    tile_total = every_tile.shape[0]
    rows = patch_count * RD
    per_owner = tile_total // patch_count
    per_frame = per_owner // FD
    owner = table // per_owner
    spot = table % per_owner
    dest = (spot // per_frame) * (tile_total // FD) + owner * per_frame + spot % per_frame
    slots = jnp.arange(tile_total, dtype=jnp.int32)
    one_hot = (slots[:, None] == dest[None, :]).astype(jnp.bfloat16)
    placed = jnp.dot(
        one_hot, every_tile.reshape(tile_total, -1), preferred_element_type=jnp.float32
    ).astype(jnp.bfloat16)
    first = jnp.reshape(patch_index * RD - 1, (1,)).astype(jnp.int32)
    mixed_own, activated = attend_frames(
        first, placed.reshape(FD, tile_total // FD, -1), (RD + 2) * W, w_query, w_keyval
    )
    activated = activated.reshape(FD, RD + 2, W, C)
    to_next = timed_conv(activated, conv_weight[:2], (0, 1)).astype(jnp.bfloat16)
    pairs = [(i, i + 1) for i in range(span_count - 1)]
    from_prev = lax.ppermute(to_next, "span", pairs)
    own_sum = timed_conv(activated, conv_weight[1:], (1, 0))
    out_width = conv_weight.shape[-1]
    own_rows = mixed_own.reshape(FD, RD, W, C)
    own_channels = lax.dynamic_slice_in_dim(own_rows, chan_index * out_width, out_width, 3)
    base = lax.optimization_barrier(own_channels.astype(jnp.float32) + own_sum)
    return (base + from_prev.astype(jnp.float32)).astype(jnp.bfloat16)


def solution(mesh):
    placed = (
        P(("clips", "span"), "patch", None, None),
        P(("clips", "span"), None),
        P(),
        P(),
        P(None, None, None, None, "chan"),
    )
    return jax.shard_map(
        local,
        mesh=mesh,
        in_specs=placed,
        out_specs=P(("clips", "span"), "patch", None, "chan"),
        check_vma=False,
    )
```

```python
import math

import jax
import jax.numpy as jnp
from jax import lax
from jax.experimental import pallas as pl
from jax.experimental.pallas import tpu as pltpu
from jax.sharding import PartitionSpec as P

C = 384
W = 64
RD = 2
FD = 2
KEY_BLOCK = 512


epsilon = 1e-06


def scaled_rms(values):
    wide = values.astype(jnp.float32)
    return wide / jnp.sqrt(jnp.mean(wide * wide, axis=-1, keepdims=True) + epsilon)


def attention_kernel(first_ref, cells_ref, wq_ref, wkv_ref, mixed_ref, act_ref):
    for frame in range(cells_ref.shape[0]):
        attend_frame(first_ref, cells_ref, wq_ref, wkv_ref, mixed_ref, act_ref, frame)


def attend_frame(first_ref, cells_ref, wq_ref, wkv_ref, mixed_ref, act_ref, frame):
    width = wq_ref.shape[0]
    scale = 1.0 / math.sqrt(width)
    count = cells_ref.shape[1]
    own = mixed_ref.shape[1]
    line = (act_ref.shape[1] - own) // 2
    frame_rows = count // line
    first = first_ref[0]
    top = jnp.maximum(first, 0) * line
    below = jnp.minimum(first + 1 + own // line, frame_rows - 1) * line
    feats = jnp.concatenate(
        [
            cells_ref[frame, pl.ds(top, line), :],
            cells_ref[frame, pl.ds((first + 1) * line, own), :],
            cells_ref[frame, pl.ds(below, line), :],
        ],
        axis=0,
    ).astype(jnp.float32)
    queries = jnp.dot(
        scaled_rms(feats).astype(jnp.bfloat16), wq_ref[...], preferred_element_type=jnp.float32
    ).astype(jnp.bfloat16)
    block = min(count, KEY_BLOCK)

    def fold(step, carry):
        run_max, run_total, run_acc = carry
        cells = cells_ref[frame, pl.ds(step * block, block), :]
        keyvals = jnp.dot(
            scaled_rms(cells).astype(jnp.bfloat16), wkv_ref[...], preferred_element_type=jnp.float32
        ).astype(jnp.bfloat16)
        scores = (
            lax.dot_general(
                queries,
                keyvals[:, :width],
                (((1,), (1,)), ((), ())),
                preferred_element_type=jnp.float32,
            )
            * scale
        )
        new_max = jnp.maximum(run_max, jnp.max(scores, axis=-1, keepdims=True))
        factor = jnp.exp(run_max - new_max)
        powers = jnp.exp(scores - new_max)
        run_total = run_total * factor + jnp.sum(powers, axis=-1, keepdims=True)
        run_acc = run_acc * factor + jnp.dot(
            powers.astype(jnp.bfloat16), keyvals[:, width:], preferred_element_type=jnp.float32
        )
        return new_max, run_total, run_acc

    rows = feats.shape[0]
    carry = (
        jnp.full((rows, 1), -jnp.inf, jnp.float32),
        jnp.zeros((rows, 1), jnp.float32),
        jnp.zeros((rows, width), jnp.float32),
    )
    for step in range(count // block):
        carry = fold(step, carry)
    _, run_total, run_acc = carry
    mixed = (feats + run_acc / run_total).astype(jnp.bfloat16)
    mixed_ref[frame] = mixed[line : line + own]
    normed = scaled_rms(mixed)
    row_of = lax.broadcasted_iota(jnp.int32, (rows, width), 0) // line + first
    inside = (row_of >= 0) & (row_of < frame_rows)
    act_ref[frame] = jnp.where(inside, normed / (1.0 + jnp.exp(-normed)), 0.0).astype(jnp.bfloat16)


def attend_frames(first, cells, ext_rows, w_query, w_keyval):
    frames, count, width = cells.shape
    own = ext_rows - 2 * (ext_rows // (RD + 2))
    fixed = lambda f, first_ref: (0, 0)
    per_frame = lambda f, first_ref: (f, 0, 0)
    grid_spec = pltpu.PrefetchScalarGridSpec(
        num_scalar_prefetch=1,
        grid=(1,),
        in_specs=[
            pl.BlockSpec((frames, count, width), per_frame),
            pl.BlockSpec(w_query.shape, fixed),
            pl.BlockSpec(w_keyval.shape, fixed),
        ],
        out_specs=[
            pl.BlockSpec((frames, own, width), per_frame),
            pl.BlockSpec((frames, ext_rows, width), per_frame),
        ],
    )
    block_bytes = count * width * 2
    return pl.pallas_call(
        attention_kernel,
        grid_spec=grid_spec,
        compiler_params=pltpu.CompilerParams(vmem_limit_bytes=6 * frames * block_bytes + (6 << 20)),
        out_shape=[
            jax.ShapeDtypeStruct((frames, own, width), jnp.bfloat16),
            jax.ShapeDtypeStruct((frames, ext_rows, width), jnp.bfloat16),
        ],
    )(first, cells, w_query, w_keyval)


def timed_conv(frames, kernel, time_pad):
    return lax.conv_general_dilated(
        frames[None],
        kernel,
        (1, 1, 1),
        (time_pad, (0, 0), (1, 1)),
        dimension_numbers=("NDHWC", "DHWIO", "NDHWC"),
        preferred_element_type=jnp.float32,
    )[0]


def local(latent_tiles, route, w_query, w_keyval, conv_weight):
    patch_count = lax.axis_size("patch")
    patch_index = lax.axis_index("patch")
    chan_count = lax.axis_size("chan")
    chan_index = lax.axis_index("chan")
    span_count = lax.axis_size("span")
    table = route[0]
    block = latent_tiles.shape[1]
    share = block // chan_count
    own_share = lax.dynamic_slice_in_dim(latent_tiles, chan_index * share, share, 1)
    every_tile = lax.all_gather(own_share, ("patch", "chan"), axis=1, tiled=True)[0]
    tile_total = every_tile.shape[0]
    rows = patch_count * RD
    per_owner = tile_total // patch_count
    per_frame = per_owner // FD
    owner = table // per_owner
    spot = table % per_owner
    dest = (spot // per_frame) * (tile_total // FD) + owner * per_frame + spot % per_frame
    slots = jnp.arange(tile_total, dtype=jnp.int32)
    one_hot = (slots[:, None] == dest[None, :]).astype(jnp.bfloat16)
    placed = jnp.dot(
        one_hot, every_tile.reshape(tile_total, -1), preferred_element_type=jnp.float32
    ).astype(jnp.bfloat16)
    whole = placed.reshape(FD, rows, W, C)
    first = jnp.reshape(patch_index * RD - 1, (1,)).astype(jnp.int32)
    mixed_own, activated = attend_frames(
        first, whole.reshape(FD, rows * W, C), (RD + 2) * W, w_query, w_keyval
    )
    activated = activated.reshape(FD, RD + 2, W, C)
    both_taps = timed_conv(activated, conv_weight[:2], (0, 0))
    last_tap = timed_conv(activated[1:], conv_weight[:1], (0, 0))
    to_next = jnp.concatenate([both_taps, last_tap]).astype(jnp.bfloat16)
    pairs = [(i, i + 1) for i in range(span_count - 1)]
    from_prev = lax.ppermute(to_next, "span", pairs)
    own_sum = timed_conv(activated, conv_weight[1:], (1, 0))
    out_width = conv_weight.shape[-1]
    own_rows = mixed_own.reshape(FD, RD, W, C)
    own_channels = lax.dynamic_slice_in_dim(own_rows, chan_index * out_width, out_width, 3)
    base = lax.optimization_barrier(own_channels.astype(jnp.float32) + own_sum)
    return (base + from_prev.astype(jnp.float32)).astype(jnp.bfloat16)


def solution(mesh):
    placed = (
        P(("clips", "span"), "patch", None, None),
        P(("clips", "span"), None),
        P(),
        P(),
        P(None, None, None, None, "chan"),
    )
    return jax.shard_map(
        local,
        mesh=mesh,
        in_specs=placed,
        out_specs=P(("clips", "span"), "patch", None, "chan"),
        check_vma=False,
    )
```

```python
import math

import jax
import jax.numpy as jnp
from jax import lax
from jax.experimental import pallas as pl
from jax.experimental.pallas import tpu as pltpu
from jax.sharding import PartitionSpec as P

C = 384
W = 64
RD = 2
FD = 2
KEY_BLOCK = 512


epsilon = 1e-06


def scaled_rms(values):
    wide = values.astype(jnp.float32)
    return wide / jnp.sqrt(jnp.mean(wide * wide, axis=-1, keepdims=True) + epsilon)


def attention_kernel(first_ref, cells_ref, wq_ref, wkv_ref, mixed_ref, act_ref):
    for frame in range(cells_ref.shape[0]):
        attend_frame(first_ref, cells_ref, wq_ref, wkv_ref, mixed_ref, act_ref, frame)


def attend_frame(first_ref, cells_ref, wq_ref, wkv_ref, mixed_ref, act_ref, frame):
    width = wq_ref.shape[0]
    scale = 1.0 / math.sqrt(width)
    count = cells_ref.shape[1]
    own = mixed_ref.shape[1]
    line = (act_ref.shape[1] - own) // 2
    frame_rows = count // line
    first = first_ref[0]
    top = jnp.maximum(first, 0) * line
    below = jnp.minimum(first + 1 + own // line, frame_rows - 1) * line
    feats = jnp.concatenate(
        [
            cells_ref[frame, pl.ds(top, line), :],
            cells_ref[frame, pl.ds((first + 1) * line, own), :],
            cells_ref[frame, pl.ds(below, line), :],
        ],
        axis=0,
    ).astype(jnp.float32)
    queries = jnp.dot(
        scaled_rms(feats).astype(jnp.bfloat16), wq_ref[...], preferred_element_type=jnp.float32
    ).astype(jnp.bfloat16)
    block = min(count, KEY_BLOCK)

    def fold(step, carry):
        run_max, run_total, run_acc = carry
        cells = cells_ref[frame, pl.ds(step * block, block), :]
        keyvals = jnp.dot(
            scaled_rms(cells).astype(jnp.bfloat16), wkv_ref[...], preferred_element_type=jnp.float32
        ).astype(jnp.bfloat16)
        scores = (
            lax.dot_general(
                queries,
                keyvals[:, :width],
                (((1,), (1,)), ((), ())),
                preferred_element_type=jnp.float32,
            )
            * scale
        )
        new_max = jnp.maximum(run_max, jnp.max(scores, axis=-1, keepdims=True))
        factor = jnp.exp(run_max - new_max)
        powers = jnp.exp(scores - new_max)
        run_total = run_total * factor + jnp.sum(powers, axis=-1, keepdims=True)
        run_acc = run_acc * factor + jnp.dot(
            powers.astype(jnp.bfloat16), keyvals[:, width:], preferred_element_type=jnp.float32
        )
        return new_max, run_total, run_acc

    rows = feats.shape[0]
    carry = (
        jnp.full((rows, 1), -jnp.inf, jnp.float32),
        jnp.zeros((rows, 1), jnp.float32),
        jnp.zeros((rows, width), jnp.float32),
    )
    for step in range(count // block):
        carry = fold(step, carry)
    _, run_total, run_acc = carry
    mixed = (feats + run_acc / run_total).astype(jnp.bfloat16)
    mixed_ref[frame] = mixed[line : line + own]
    normed = scaled_rms(mixed)
    row_of = lax.broadcasted_iota(jnp.int32, (rows, width), 0) // line + first
    inside = (row_of >= 0) & (row_of < frame_rows)
    activated = jnp.where(inside, normed / (1.0 + jnp.exp(-normed)), 0.0).astype(jnp.bfloat16)
    band = rows // line
    target = lax.broadcasted_iota(jnp.int32, (rows, rows), 0)
    source = lax.broadcasted_iota(jnp.int32, (rows, rows), 1)
    swap = (source == (target % band) * line + target // band).astype(jnp.bfloat16)
    act_ref[frame] = jnp.dot(swap, activated, preferred_element_type=jnp.float32).astype(
        jnp.bfloat16
    )


def attend_frames(first, cells, ext_rows, w_query, w_keyval):
    frames, count, width = cells.shape
    own = ext_rows - 2 * (ext_rows // (RD + 2))
    fixed = lambda f, first_ref: (0, 0)
    per_frame = lambda f, first_ref: (f, 0, 0)
    grid_spec = pltpu.PrefetchScalarGridSpec(
        num_scalar_prefetch=1,
        grid=(1,),
        in_specs=[
            pl.BlockSpec((frames, count, width), per_frame),
            pl.BlockSpec(w_query.shape, fixed),
            pl.BlockSpec(w_keyval.shape, fixed),
        ],
        out_specs=[
            pl.BlockSpec((frames, own, width), per_frame),
            pl.BlockSpec((frames, ext_rows, width), per_frame),
        ],
    )
    block_bytes = count * width * 2
    return pl.pallas_call(
        attention_kernel,
        grid_spec=grid_spec,
        compiler_params=pltpu.CompilerParams(vmem_limit_bytes=6 * frames * block_bytes + (6 << 20)),
        out_shape=[
            jax.ShapeDtypeStruct((frames, own, width), jnp.bfloat16),
            jax.ShapeDtypeStruct((frames, ext_rows, width), jnp.bfloat16),
        ],
    )(first, cells, w_query, w_keyval)


def timed_conv(frames, kernel, time_pad):
    return lax.conv_general_dilated(
        frames[None],
        kernel,
        (1, 1, 1),
        (time_pad, (0, 0), (1, 1)),
        dimension_numbers=("NDHWC", "DHWIO", "NDHWC"),
        preferred_element_type=jnp.float32,
    )[0]


def local(latent_tiles, route, w_query, w_keyval, conv_weight):
    patch_count = lax.axis_size("patch")
    patch_index = lax.axis_index("patch")
    chan_count = lax.axis_size("chan")
    chan_index = lax.axis_index("chan")
    span_count = lax.axis_size("span")
    table = route[0]
    block = latent_tiles.shape[1]
    share = block // chan_count
    own_share = lax.dynamic_slice_in_dim(latent_tiles, chan_index * share, share, 1)
    every_tile = lax.all_gather(own_share, ("patch", "chan"), axis=1, tiled=True)[0]
    tile_total = every_tile.shape[0]
    rows = patch_count * RD
    per_owner = tile_total // patch_count
    per_frame = per_owner // FD
    owner = table // per_owner
    spot = table % per_owner
    dest = (spot // per_frame) * (tile_total // FD) + owner * per_frame + spot % per_frame
    slots = jnp.arange(tile_total, dtype=jnp.int32)
    one_hot = (slots[:, None] == dest[None, :]).astype(jnp.bfloat16)
    placed = jnp.dot(
        one_hot, every_tile.reshape(tile_total, -1), preferred_element_type=jnp.float32
    ).astype(jnp.bfloat16)
    whole = placed.reshape(FD, rows, W, C)
    first = jnp.reshape(patch_index * RD - 1, (1,)).astype(jnp.int32)
    mixed_own, activated = attend_frames(
        first, whole.reshape(FD, rows * W, C), (RD + 2) * W, w_query, w_keyval
    )
    activated = activated.reshape(FD, W, RD + 2, C).transpose(0, 2, 1, 3)
    to_next = timed_conv(activated, conv_weight[:2], (0, 1)).astype(jnp.bfloat16)
    pairs = [(i, i + 1) for i in range(span_count - 1)]
    from_prev = lax.ppermute(to_next, "span", pairs)
    own_sum = timed_conv(activated, conv_weight[1:], (1, 0))
    out_width = conv_weight.shape[-1]
    own_rows = mixed_own.reshape(FD, RD, W, C)
    own_channels = lax.dynamic_slice_in_dim(own_rows, chan_index * out_width, out_width, 3)
    base = lax.optimization_barrier(own_channels.astype(jnp.float32) + own_sum)
    return (base + from_prev.astype(jnp.float32)).astype(jnp.bfloat16)


def solution(mesh):
    placed = (
        P(("clips", "span"), "patch", None, None),
        P(("clips", "span"), None),
        P(),
        P(),
        P(None, None, None, None, "chan"),
    )
    return jax.shard_map(
        local,
        mesh=mesh,
        in_specs=placed,
        out_specs=P(("clips", "span"), "patch", None, "chan"),
        check_vma=False,
    )
```

```python
import math

import jax
import jax.numpy as jnp
from jax import lax
from jax.experimental import pallas as pl
from jax.experimental.pallas import tpu as pltpu
from jax.sharding import PartitionSpec as P

C = 384
W = 64
RD = 2
FD = 2
KEY_BLOCK = 512


epsilon = 1e-06


def scaled_rms(values):
    wide = values.astype(jnp.float32)
    return wide / jnp.sqrt(jnp.mean(wide * wide, axis=-1, keepdims=True) + epsilon)


def attention_kernel(first_ref, cells_ref, wq_ref, wkv_ref, mixed_ref, act_ref):
    frames, count, width = cells_ref.shape
    shared = None
    if count <= KEY_BLOCK:
        every = cells_ref[...].reshape(frames * count, width)
        shared = jnp.dot(
            scaled_rms(every).astype(jnp.bfloat16), wkv_ref[...], preferred_element_type=jnp.float32
        ).astype(jnp.bfloat16)
    for frame in range(frames):
        attend_frame(first_ref, cells_ref, wq_ref, wkv_ref, mixed_ref, act_ref, frame, shared)


def attend_frame(first_ref, cells_ref, wq_ref, wkv_ref, mixed_ref, act_ref, frame, shared):
    width = wq_ref.shape[0]
    scale = 1.0 / math.sqrt(width)
    count = cells_ref.shape[1]
    own = mixed_ref.shape[1]
    line = (act_ref.shape[1] - own) // 2
    frame_rows = count // line
    first = first_ref[0]
    top = jnp.maximum(first, 0) * line
    below = jnp.minimum(first + 1 + own // line, frame_rows - 1) * line
    feats = jnp.concatenate(
        [
            cells_ref[frame, pl.ds(top, line), :],
            cells_ref[frame, pl.ds((first + 1) * line, own), :],
            cells_ref[frame, pl.ds(below, line), :],
        ],
        axis=0,
    ).astype(jnp.float32)
    queries = jnp.dot(
        scaled_rms(feats).astype(jnp.bfloat16), wq_ref[...], preferred_element_type=jnp.float32
    ).astype(jnp.bfloat16)
    block = min(count, KEY_BLOCK)

    def fold(step, carry):
        run_max, run_total, run_acc = carry
        if shared is None:
            cells = cells_ref[frame, pl.ds(step * block, block), :]
            keyvals = jnp.dot(
                scaled_rms(cells).astype(jnp.bfloat16),
                wkv_ref[...],
                preferred_element_type=jnp.float32,
            ).astype(jnp.bfloat16)
        else:
            keyvals = shared[frame * count : (frame + 1) * count]
        scores = (
            lax.dot_general(
                queries,
                keyvals[:, :width],
                (((1,), (1,)), ((), ())),
                preferred_element_type=jnp.float32,
            )
            * scale
        )
        new_max = jnp.maximum(run_max, jnp.max(scores, axis=-1, keepdims=True))
        factor = jnp.exp(run_max - new_max)
        powers = jnp.exp(scores - new_max)
        run_total = run_total * factor + jnp.sum(powers, axis=-1, keepdims=True)
        run_acc = run_acc * factor + jnp.dot(
            powers.astype(jnp.bfloat16), keyvals[:, width:], preferred_element_type=jnp.float32
        )
        return new_max, run_total, run_acc

    rows = feats.shape[0]
    carry = (
        jnp.full((rows, 1), -jnp.inf, jnp.float32),
        jnp.zeros((rows, 1), jnp.float32),
        jnp.zeros((rows, width), jnp.float32),
    )
    for step in range(count // block):
        carry = fold(step, carry)
    _, run_total, run_acc = carry
    mixed = (feats + run_acc / run_total).astype(jnp.bfloat16)
    mixed_ref[frame] = mixed[line : line + own]
    normed = scaled_rms(mixed)
    row_of = lax.broadcasted_iota(jnp.int32, (rows, width), 0) // line + first
    inside = (row_of >= 0) & (row_of < frame_rows)
    act_ref[frame] = jnp.where(inside, normed / (1.0 + jnp.exp(-normed)), 0.0).astype(jnp.bfloat16)


def attend_frames(first, cells, ext_rows, w_query, w_keyval):
    frames, count, width = cells.shape
    own = ext_rows - 2 * (ext_rows // (RD + 2))
    fixed = lambda f, first_ref: (0, 0)
    per_frame = lambda f, first_ref: (f, 0, 0)
    grid_spec = pltpu.PrefetchScalarGridSpec(
        num_scalar_prefetch=1,
        grid=(1,),
        in_specs=[
            pl.BlockSpec((frames, count, width), per_frame),
            pl.BlockSpec(w_query.shape, fixed),
            pl.BlockSpec(w_keyval.shape, fixed),
        ],
        out_specs=[
            pl.BlockSpec((frames, own, width), per_frame),
            pl.BlockSpec((frames, ext_rows, width), per_frame),
        ],
    )
    block_bytes = count * width * 2
    return pl.pallas_call(
        attention_kernel,
        grid_spec=grid_spec,
        compiler_params=pltpu.CompilerParams(vmem_limit_bytes=6 * frames * block_bytes + (6 << 20)),
        out_shape=[
            jax.ShapeDtypeStruct((frames, own, width), jnp.bfloat16),
            jax.ShapeDtypeStruct((frames, ext_rows, width), jnp.bfloat16),
        ],
    )(first, cells, w_query, w_keyval)


def timed_conv(frames, kernel, time_pad):
    return lax.conv_general_dilated(
        frames[None],
        kernel,
        (1, 1, 1),
        (time_pad, (0, 0), (1, 1)),
        dimension_numbers=("NDHWC", "DHWIO", "NDHWC"),
        preferred_element_type=jnp.float32,
    )[0]


def local(latent_tiles, route, w_query, w_keyval, conv_weight):
    patch_count = lax.axis_size("patch")
    patch_index = lax.axis_index("patch")
    chan_count = lax.axis_size("chan")
    chan_index = lax.axis_index("chan")
    span_count = lax.axis_size("span")
    table = route[0]
    block = latent_tiles.shape[1]
    share = block // chan_count
    own_share = lax.dynamic_slice_in_dim(latent_tiles, chan_index * share, share, 1)
    every_tile = lax.all_gather(own_share, ("patch", "chan"), axis=1, tiled=True)[0]
    tile_total = every_tile.shape[0]
    rows = patch_count * RD
    per_owner = tile_total // patch_count
    per_frame = per_owner // FD
    owner = table // per_owner
    spot = table % per_owner
    dest = (spot // per_frame) * (tile_total // FD) + owner * per_frame + spot % per_frame
    slots = jnp.arange(tile_total, dtype=jnp.int32)
    one_hot = (slots[:, None] == dest[None, :]).astype(jnp.bfloat16)
    placed = jnp.dot(
        one_hot, every_tile.reshape(tile_total, -1), preferred_element_type=jnp.float32
    ).astype(jnp.bfloat16)
    whole = placed.reshape(FD, rows, W, C)
    first = jnp.reshape(patch_index * RD - 1, (1,)).astype(jnp.int32)
    mixed_own, activated = attend_frames(
        first, whole.reshape(FD, rows * W, C), (RD + 2) * W, w_query, w_keyval
    )
    activated = activated.reshape(FD, RD + 2, W, C)
    to_next = timed_conv(activated, conv_weight[:2], (0, 1)).astype(jnp.bfloat16)
    pairs = [(i, i + 1) for i in range(span_count - 1)]
    from_prev = lax.ppermute(to_next, "span", pairs)
    own_sum = timed_conv(activated, conv_weight[1:], (1, 0))
    out_width = conv_weight.shape[-1]
    own_rows = mixed_own.reshape(FD, RD, W, C)
    own_channels = lax.dynamic_slice_in_dim(own_rows, chan_index * out_width, out_width, 3)
    base = lax.optimization_barrier(own_channels.astype(jnp.float32) + own_sum)
    return (base + from_prev.astype(jnp.float32)).astype(jnp.bfloat16)


def solution(mesh):
    placed = (
        P(("clips", "span"), "patch", None, None),
        P(("clips", "span"), None),
        P(),
        P(),
        P(None, None, None, None, "chan"),
    )
    return jax.shard_map(
        local,
        mesh=mesh,
        in_specs=placed,
        out_specs=P(("clips", "span"), "patch", None, "chan"),
        check_vma=False,
    )
```

```python
import math

import jax
import jax.numpy as jnp
from jax import lax
from jax.experimental import pallas as pl
from jax.experimental.pallas import tpu as pltpu
from jax.sharding import PartitionSpec as P

C = 384
W = 64
RD = 2
FD = 2
KEY_BLOCK = 512


epsilon = 1e-06


def scaled_rms(values):
    wide = values.astype(jnp.float32)
    return wide / jnp.sqrt(jnp.mean(wide * wide, axis=-1, keepdims=True) + epsilon)


def attention_kernel(first_ref, cells_ref, wq_ref, wkv_ref, mixed_ref, act_ref):
    frames, count, width = cells_ref.shape
    shared = None
    if count <= KEY_BLOCK:
        every = cells_ref[...].reshape(frames * count, width)
        shared = jnp.dot(
            scaled_rms(every).astype(jnp.bfloat16), wkv_ref[...], preferred_element_type=jnp.float32
        ).astype(jnp.bfloat16)
    picked = [query_rows(first_ref, cells_ref, mixed_ref, act_ref, f) for f in range(frames)]
    rows = picked[0].shape[0]
    asked = jnp.dot(
        scaled_rms(jnp.concatenate(picked, axis=0)).astype(jnp.bfloat16),
        wq_ref[...],
        preferred_element_type=jnp.float32,
    ).astype(jnp.bfloat16)
    for frame in range(frames):
        queries = asked[frame * rows : (frame + 1) * rows]
        attend_frame(
            first_ref, cells_ref, wkv_ref, mixed_ref, act_ref, frame, shared, picked[frame], queries
        )


def query_rows(first_ref, cells_ref, mixed_ref, act_ref, frame):
    count = cells_ref.shape[1]
    own = mixed_ref.shape[1]
    line = (act_ref.shape[1] - own) // 2
    frame_rows = count // line
    first = first_ref[0]
    top = jnp.maximum(first, 0) * line
    below = jnp.minimum(first + 1 + own // line, frame_rows - 1) * line
    return jnp.concatenate(
        [
            cells_ref[frame, pl.ds(top, line), :],
            cells_ref[frame, pl.ds((first + 1) * line, own), :],
            cells_ref[frame, pl.ds(below, line), :],
        ],
        axis=0,
    ).astype(jnp.float32)


def attend_frame(
    first_ref, cells_ref, wkv_ref, mixed_ref, act_ref, frame, shared, feats, queries
):
    width = cells_ref.shape[2]
    scale = 1.0 / math.sqrt(width)
    count = cells_ref.shape[1]
    own = mixed_ref.shape[1]
    line = (act_ref.shape[1] - own) // 2
    frame_rows = count // line
    first = first_ref[0]
    block = min(count, KEY_BLOCK)

    def fold(step, carry):
        run_max, run_total, run_acc = carry
        if shared is None:
            cells = cells_ref[frame, pl.ds(step * block, block), :]
            keyvals = jnp.dot(
                scaled_rms(cells).astype(jnp.bfloat16),
                wkv_ref[...],
                preferred_element_type=jnp.float32,
            ).astype(jnp.bfloat16)
        else:
            keyvals = shared[frame * count : (frame + 1) * count]
        scores = (
            lax.dot_general(
                queries,
                keyvals[:, :width],
                (((1,), (1,)), ((), ())),
                preferred_element_type=jnp.float32,
            )
            * scale
        )
        new_max = jnp.maximum(run_max, jnp.max(scores, axis=-1, keepdims=True))
        factor = jnp.exp(run_max - new_max)
        powers = jnp.exp(scores - new_max)
        run_total = run_total * factor + jnp.sum(powers, axis=-1, keepdims=True)
        run_acc = run_acc * factor + jnp.dot(
            powers.astype(jnp.bfloat16), keyvals[:, width:], preferred_element_type=jnp.float32
        )
        return new_max, run_total, run_acc

    rows = feats.shape[0]
    carry = (
        jnp.full((rows, 1), -jnp.inf, jnp.float32),
        jnp.zeros((rows, 1), jnp.float32),
        jnp.zeros((rows, width), jnp.float32),
    )
    for step in range(count // block):
        carry = fold(step, carry)
    _, run_total, run_acc = carry
    mixed = (feats + run_acc / run_total).astype(jnp.bfloat16)
    mixed_ref[frame] = mixed[line : line + own]
    normed = scaled_rms(mixed)
    row_of = lax.broadcasted_iota(jnp.int32, (rows, width), 0) // line + first
    inside = (row_of >= 0) & (row_of < frame_rows)
    act_ref[frame] = jnp.where(inside, normed / (1.0 + jnp.exp(-normed)), 0.0).astype(jnp.bfloat16)


def attend_frames(first, cells, ext_rows, w_query, w_keyval):
    frames, count, width = cells.shape
    own = ext_rows - 2 * (ext_rows // (RD + 2))
    fixed = lambda f, first_ref: (0, 0)
    per_frame = lambda f, first_ref: (f, 0, 0)
    grid_spec = pltpu.PrefetchScalarGridSpec(
        num_scalar_prefetch=1,
        grid=(1,),
        in_specs=[
            pl.BlockSpec((frames, count, width), per_frame),
            pl.BlockSpec(w_query.shape, fixed),
            pl.BlockSpec(w_keyval.shape, fixed),
        ],
        out_specs=[
            pl.BlockSpec((frames, own, width), per_frame),
            pl.BlockSpec((frames, ext_rows, width), per_frame),
        ],
    )
    block_bytes = count * width * 2
    return pl.pallas_call(
        attention_kernel,
        grid_spec=grid_spec,
        compiler_params=pltpu.CompilerParams(vmem_limit_bytes=6 * frames * block_bytes + (6 << 20)),
        out_shape=[
            jax.ShapeDtypeStruct((frames, own, width), jnp.bfloat16),
            jax.ShapeDtypeStruct((frames, ext_rows, width), jnp.bfloat16),
        ],
    )(first, cells, w_query, w_keyval)


def timed_conv(frames, kernel, time_pad):
    return lax.conv_general_dilated(
        frames[None],
        kernel,
        (1, 1, 1),
        (time_pad, (0, 0), (1, 1)),
        dimension_numbers=("NDHWC", "DHWIO", "NDHWC"),
        preferred_element_type=jnp.float32,
    )[0]


def local(latent_tiles, route, w_query, w_keyval, conv_weight):
    patch_count = lax.axis_size("patch")
    patch_index = lax.axis_index("patch")
    chan_count = lax.axis_size("chan")
    chan_index = lax.axis_index("chan")
    span_count = lax.axis_size("span")
    table = route[0]
    block = latent_tiles.shape[1]
    share = block // chan_count
    own_share = lax.dynamic_slice_in_dim(latent_tiles, chan_index * share, share, 1)
    every_tile = lax.all_gather(own_share, ("patch", "chan"), axis=1, tiled=True)[0]
    tile_total = every_tile.shape[0]
    rows = patch_count * RD
    per_owner = tile_total // patch_count
    per_frame = per_owner // FD
    owner = table // per_owner
    spot = table % per_owner
    dest = (spot // per_frame) * (tile_total // FD) + owner * per_frame + spot % per_frame
    slots = jnp.arange(tile_total, dtype=jnp.int32)
    one_hot = (slots[:, None] == dest[None, :]).astype(jnp.bfloat16)
    placed = jnp.dot(
        one_hot, every_tile.reshape(tile_total, -1), preferred_element_type=jnp.float32
    ).astype(jnp.bfloat16)
    whole = placed.reshape(FD, rows, W, C)
    first = jnp.reshape(patch_index * RD - 1, (1,)).astype(jnp.int32)
    mixed_own, activated = attend_frames(
        first, whole.reshape(FD, rows * W, C), (RD + 2) * W, w_query, w_keyval
    )
    activated = activated.reshape(FD, RD + 2, W, C)
    to_next = timed_conv(activated, conv_weight[:2], (0, 1)).astype(jnp.bfloat16)
    pairs = [(i, i + 1) for i in range(span_count - 1)]
    from_prev = lax.ppermute(to_next, "span", pairs)
    own_sum = timed_conv(activated, conv_weight[1:], (1, 0))
    out_width = conv_weight.shape[-1]
    own_rows = mixed_own.reshape(FD, RD, W, C)
    own_channels = lax.dynamic_slice_in_dim(own_rows, chan_index * out_width, out_width, 3)
    base = lax.optimization_barrier(own_channels.astype(jnp.float32) + own_sum)
    return (base + from_prev.astype(jnp.float32)).astype(jnp.bfloat16)


def solution(mesh):
    placed = (
        P(("clips", "span"), "patch", None, None),
        P(("clips", "span"), None),
        P(),
        P(),
        P(None, None, None, None, "chan"),
    )
    return jax.shard_map(
        local,
        mesh=mesh,
        in_specs=placed,
        out_specs=P(("clips", "span"), "patch", None, "chan"),
        check_vma=False,
    )
```
